256 devices in a mesh: kv: 8 (over y, z_lo), blk: 32 (over x, z_hi, core).
Axes of the slice: x: 4, y: 4, z: 8 (z_hi: 4, z_lo: 2; z = z_hi * 2 + z_lo), core: 2. Of those that a mesh axis runs over, the one named last changes fastest.
Arguments:
- suffix_query: bfloat16 [6144, 4096], P('blk', 'kv'), may hold values from -6 to 6
- suffix_key_value: bfloat16 [2, 6144, 2048], P(None, 'blk', 'kv'), may hold values from -6 to 6
- suffix_resid: bfloat16 [6144, 4608], P('blk', 'kv'), may hold values from -6 to 6
- decode_query_rows: bfloat16 [64, 4096], P('blk', 'kv'), may hold values from -6 to 6
- decode_key_value: bfloat16 [2, 64, 2048], P(None, 'blk', 'kv'), may hold values from -6 to 6
- decode_resid: bfloat16 [64, 4608], P('blk', 'kv'), may hold values from -6 to 6
- out_weight: bfloat16 [4096, 4608], P('kv'), may hold values from -1.125 to 1.125
- post_gain: float32 [4608], P('kv'), may hold values from 0.1 to 1.9
- prefix_page_store: bfloat16 [2, 96, 128, 2048], P(None, 'blk', None, 'kv'), may hold values from -6 to 6
- prefix_table: int32 [96], replicated, may hold values from 0 to 95, each once
- decode_page_store: bfloat16 [2, 512, 128, 2048], P(None, 'blk', None, 'kv'), may hold values from -6 to 6
- page_table: int32 [512], replicated, may hold values from 0 to 511, each once
- suffix_lengths: int32 [16], replicated, may hold values from 1 to 768, 6144 in all
- suffix_prefix: int32 [16], replicated, may hold values from 0 to 3
- decode_ages: int32 [64], replicated, may hold values from 1 to 1023, as said below
Outputs:
- suffix_hidden: bfloat16 [6144, 4608], P('blk', 'kv')
- decode_hidden: bfloat16 [64, 4608], P('blk', 'kv')
- new_cache: bfloat16 [2, 512, 128, 2048], P(None, 'blk', None, 'kv')
The draws below stay inside these ranges and needn't reach their ends.
Inputs may be any that keep to these rules, and one draw needn't show every extreme that they name: `page_table`: every page of the decode pool is named once. `prefix_table`: every page of the prefix pool is named once. `suffix_lengths`: the lengths sum to 6144; one is exactly 768. `decode_ages`: some slot has age 1024 - 1.
All inputs are finite; a program needn't handle non-finite values.
Results may differ from the reference program's by a relative error of at most 0.024.
Values may be sent and summed in bfloat16 or wider, within the bound.
No kernel may reach another device: no remote copies, remote signals or barrier semaphores. Data moves between devices by JAX's collectives and lax.ppermute only.
A program may use at most 128 MiB of HBM per device.

```python
import math
import jax
import jax.numpy as jnp
import numpy as np
from jax import lax

D = 4608
QUERY_HEADS = 32
KEY_VALUE_HEADS = 16
HEAD_SIZE = 128
PAGE_TOKENS = 128
PREFIX_COUNT = 4
NSUF = 16
PREFIX_LENGTH = 3072
SUF_DEV = 192
SLOT_CAPACITY = 1024
SUFFIX_TOKENS = 6144
DECODE_SLOTS = 64
DECODE_PAGES = 512
PREFIX_PAGES = 96


def draw_out_weight(key, part):
    fan_in = QUERY_HEADS * HEAD_SIZE
    base = jnp.clip(jax.random.normal(key, (QUERY_HEADS * HEAD_SIZE, D), jnp.float32), -6.0, 6.0)
    column = jnp.arange(D, dtype=jnp.float32) / D
    rough = jax.random.uniform(jax.random.fold_in(key, 11), (D,), jnp.float32)
    spread = jnp.exp(1.2 * column + 1.2 * rough)
    return (base * spread[None, :] * (0.4 / fan_in ** 0.5)).astype(jnp.bfloat16)


def draw_decode_ages(key, part):
    ages = jax.random.randint(key, (DECODE_SLOTS,), 1, SLOT_CAPACITY, dtype=jnp.int32)
    target = jax.random.randint(jax.random.fold_in(key, 3), (), 0, DECODE_SLOTS, dtype=jnp.int32)
    return ages.at[target].set(SLOT_CAPACITY - 1)


def set_ends(values, own_key, smallest, top_value):
    longest = values.shape.index(max(values.shape))
    spots = []
    for shift in (0, 1):
        where = [jax.random.randint(jax.random.fold_in(own_key, axis), (), 0, length) for axis, length in enumerate(values.shape)]
        where[longest] = (where[longest] + shift) % values.shape[longest]
        spots.append(tuple(where))
    return values.at[spots[0]].set(smallest).at[spots[1]].set(top_value)


def block_scale(key, extent, shards, low, top_value):
    def one(position, blocks):
        heights = jax.random.uniform(jax.random.fold_in(jax.random.fold_in(key, 6), position), (blocks,), jnp.float32, low / len(shards), top_value / len(shards))
        return jnp.repeat(jnp.exp(heights), extent[position] // blocks).reshape((-1,) + (1,) * (len(extent) - position - 1))

    factor_of = one(*shards[0])
    for cut in shards[1:]:
        factor_of = factor_of * one(*cut)
    return factor_of


def rank_bounds(count, skew):
    portions = [(1 << 20) // math.isqrt(rank ** skew) + 1 for rank in range(1, count + 1)]
    width = 1 + sum(portions) // (1 << 30)
    return np.cumsum(np.array([max(1, weight // width) for weight in portions]))


def ranked_ids(own_key, shape, amount, slope):
    table = rank_bounds(amount, slope)
    ticket = jax.random.randint(jax.random.fold_in(own_key, 1), shape, 0, int(table[amount - 1]))
    grade = jnp.searchsorted(jnp.asarray(table, jnp.int32), ticket, side="right")
    return jax.random.permutation(jax.random.fold_in(own_key, 2), amount)[grade].astype(jnp.int32)


def profile(count, total, most, lean):
    portions = [(1 << 20) // math.isqrt(grade ** lean) + 1 for grade in range(2, count + 1)]
    rest, holding = total - most - (count - 1), [1] * (count - 1)
    while rest > 0:
        candidates = [i for i in range(count - 1) if holding[i] < most]
        mass, budget = sum([portions[i] for i in candidates]), rest
        for i in candidates:
            more = min(most - holding[i], max(1, budget * portions[i] // mass), rest)
            holding[i] = holding[i] + more
            rest = rest - more
    return np.array([most] + holding)


def ragged(rng, amount, total, bound, slope):
    if amount == 2:
        one = jax.random.randint(rng, (), max(1, total - bound), min(bound, total - 1) + 1)
        return jnp.stack([one, total - one])
    lengths = jnp.asarray(profile(amount, total, bound, slope), jnp.int32)
    pairs = (amount - 1) // 2
    donor, taker = lengths[1:1 + 2 * pairs:2], lengths[2:2 + 2 * pairs:2]
    room = jnp.minimum(donor - 1, bound - taker)
    moved = jax.random.randint(jax.random.fold_in(rng, 1), (pairs,), 0, 1 << 20) % (room + 1)
    lengths = lengths.at[1:1 + 2 * pairs:2].set(donor - moved).at[2:2 + 2 * pairs:2].set(taker + moved)
    return lengths[jax.random.permutation(jax.random.fold_in(rng, 2), amount)]


def normal_values(stream_key, dims, width, limit, pieces=(), kind=jnp.bfloat16):
    values = jax.random.normal(stream_key, dims, jnp.float32) * width
    if len(pieces) > 0:
        values = block_scale(stream_key, dims, pieces, -0.22, 0.18) * values
    return jnp.clip(values, min=-limit, max=limit).astype(kind)


def setup_inputs(seed: int = 0) -> dict:
    key_list = jax.random.split(jax.random.key(seed), 16)
    return {
        "suffix_query": normal_values(key_list[0], (SUFFIX_TOKENS, QUERY_HEADS * HEAD_SIZE), 1.0, 6.0, ((0, 32), (1, 8))),
        "suffix_key_value": normal_values(key_list[1], (2, SUFFIX_TOKENS, KEY_VALUE_HEADS * HEAD_SIZE), 1.0, 6.0, ((1, 32), (2, 8))),
        "suffix_resid": normal_values(key_list[2], (SUFFIX_TOKENS, D), 1.0, 6.0, ((0, 32), (1, 8))),
        "decode_query_rows": normal_values(key_list[3], (DECODE_SLOTS, QUERY_HEADS * HEAD_SIZE), 1.0, 6.0, ((0, 32), (1, 8))),
        "decode_key_value": normal_values(key_list[4], (2, DECODE_SLOTS, KEY_VALUE_HEADS * HEAD_SIZE), 1.0, 6.0, ((1, 32), (2, 8))),
        "decode_resid": normal_values(key_list[5], (DECODE_SLOTS, D), 1.0, 6.0, ((0, 32), (1, 8))),
        "out_weight": draw_out_weight(jax.random.fold_in(key_list[15], 71), 0),
        "post_gain": jnp.clip(1.0 + 0.18 * jax.random.normal(key_list[7], (D,), jnp.float32), 0.1, 1.9),
        "prefix_page_store": normal_values(key_list[8], (2, PREFIX_PAGES, PAGE_TOKENS, KEY_VALUE_HEADS * HEAD_SIZE), 1.0, 6.0, ((1, 32), (3, 8))),
        "prefix_table": jax.random.permutation(key_list[9], PREFIX_PAGES).astype(jnp.int32),
        "decode_page_store": normal_values(key_list[10], (2, DECODE_PAGES, PAGE_TOKENS, KEY_VALUE_HEADS * HEAD_SIZE), 1.0, 6.0, ((1, 32), (3, 8))),
        "page_table": jax.random.permutation(key_list[11], DECODE_PAGES).astype(jnp.int32),
        "suffix_lengths": ragged(key_list[12], NSUF, SUFFIX_TOKENS, 4 * SUF_DEV, 1).astype(jnp.int32),
        "suffix_prefix": set_ends(ranked_ids(key_list[13], (NSUF,), PREFIX_COUNT, 2), jax.random.fold_in(key_list[13], 3), 0, PREFIX_COUNT - 1).astype(jnp.int32),
        "decode_ages": draw_decode_ages(jax.random.fold_in(key_list[15], 71), 0),
    }


soft_cap = 50.0
norm_eps = 1e-06

def rounded(weights):
    half = weights.astype(jnp.bfloat16)
    half = lax.optimization_barrier(half)
    return half.astype(jnp.float32)

def attend(query_rows, key_rows, value_rows, visible, q_scale):
    logits = jnp.einsum('qhgd,khd->qhgk', query_rows.astype(jnp.float32), key_rows.astype(jnp.float32)) * q_scale
    capped = soft_cap * jnp.tanh(logits / soft_cap)
    weights = jnp.where(visible[:, None, None, :], jnp.exp(capped), 0.0)
    denominator = lax.optimization_barrier(jnp.sum(weights, axis=3))
    numerator = jnp.einsum('qhgk,khd->qhgd', rounded(weights), value_rows.astype(jnp.float32))
    return (numerator, denominator)

def suffix_part(suffix_query, suffix_key_value, prefix_page_store, prefix_table, suffix_lengths, suffix_prefix):
    query_group_width = QUERY_HEADS // KEY_VALUE_HEADS
    token_extent = 4 * SUF_DEV
    q_scale = (D // QUERY_HEADS) ** (-0.5)
    per_prefix = PREFIX_LENGTH // PAGE_TOKENS
    prefix_page_list = prefix_page_store[:, prefix_table.reshape(PREFIX_COUNT, per_prefix)]
    prefix_key_rows = prefix_page_list[0].reshape(PREFIX_COUNT, PREFIX_LENGTH, KEY_VALUE_HEADS, HEAD_SIZE)
    prefix_value_rows = prefix_page_list[1].reshape(PREFIX_COUNT, PREFIX_LENGTH, KEY_VALUE_HEADS, HEAD_SIZE)
    padded_query = jnp.concatenate([suffix_query, jnp.zeros((token_extent, QUERY_HEADS * HEAD_SIZE), suffix_query.dtype)], axis=0)
    padded_query = padded_query.reshape(SUFFIX_TOKENS + token_extent, KEY_VALUE_HEADS, query_group_width, HEAD_SIZE)
    padded_key_value = jnp.concatenate([suffix_key_value, jnp.zeros((2, token_extent, KEY_VALUE_HEADS * HEAD_SIZE), suffix_key_value.dtype)], axis=1)
    padded_key_value = padded_key_value.reshape(2, SUFFIX_TOKENS + token_extent, KEY_VALUE_HEADS, HEAD_SIZE)
    suffix_ends = jnp.cumsum(suffix_lengths).astype(jnp.int32)
    starts = (suffix_ends - suffix_lengths).astype(jnp.int32)
    places = jnp.arange(token_extent, dtype=jnp.int32)
    causal = places[None, :] <= places[:, None]
    everyone = jnp.ones((token_extent, PREFIX_LENGTH), dtype=bool)

    def one_suffix(result, index):
        first = starts[index]
        length_now = suffix_lengths[index]
        owner = suffix_prefix[index]
        q_window = lax.dynamic_slice_in_dim(padded_query, first, token_extent, 0)
        k_window = lax.dynamic_slice_in_dim(padded_key_value[0], first, token_extent, 0)
        v_window = lax.dynamic_slice_in_dim(padded_key_value[1], first, token_extent, 0)
        pre_keys = lax.dynamic_index_in_dim(prefix_key_rows, owner, 0, keepdims=False)
        pre_values = lax.dynamic_index_in_dim(prefix_value_rows, owner, 0, keepdims=False)
        numer_one, denom_one = attend(q_window, pre_keys, pre_values, everyone, q_scale)
        visible = causal & (places[None, :] < length_now)
        numer_two, denom_two = attend(q_window, k_window, v_window, visible, q_scale)
        output = ((numer_one + numer_two) / (denom_one + denom_two)[..., None]).astype(jnp.bfloat16)
        result = lax.dynamic_update_slice_in_dim(result, output.reshape(token_extent, QUERY_HEADS * HEAD_SIZE), first, 0)
        return (result, None)
    result = jnp.zeros((SUFFIX_TOKENS + token_extent, QUERY_HEADS * HEAD_SIZE), jnp.bfloat16)
    result, _ = lax.scan(one_suffix, result, jnp.arange(NSUF, dtype=jnp.int32))
    return result[:SUFFIX_TOKENS]

def decode_part(decode_query_rows, decode_key_value, decode_page_store, page_table, decode_ages):
    query_group_width = QUERY_HEADS // KEY_VALUE_HEADS
    q_scale = (D // QUERY_HEADS) ** (-0.5)
    slot_pages = SLOT_CAPACITY // PAGE_TOKENS
    table = page_table.reshape(DECODE_SLOTS, slot_pages)
    slot_ids = jnp.arange(DECODE_SLOTS, dtype=jnp.int32)
    target = table[slot_ids, (decode_ages // PAGE_TOKENS).astype(jnp.int32)]
    offsets = (decode_ages % PAGE_TOKENS).astype(jnp.int32)
    refreshed_cache = decode_page_store.at[:, target, offsets].set(decode_key_value)
    query_rows = decode_query_rows.reshape(DECODE_SLOTS, KEY_VALUE_HEADS, query_group_width, HEAD_SIZE)

    def one_slot(element):
        slot_query, slot_page_map, slot_age = element
        sequence_index = refreshed_cache[:, slot_page_map].reshape(2, SLOT_CAPACITY, KEY_VALUE_HEADS, HEAD_SIZE)
        visible = (jnp.arange(SLOT_CAPACITY, dtype=jnp.int32) <= slot_age)[None, :]
        numerator, denominator = attend(slot_query[None], sequence_index[0], sequence_index[1], visible, q_scale)
        return (numerator / denominator[..., None])[0].astype(jnp.bfloat16).reshape(QUERY_HEADS * HEAD_SIZE)
    output = lax.map(one_slot, (query_rows, table, decode_ages))
    return (output, refreshed_cache)

def reference(suffix_query, suffix_key_value, suffix_resid, decode_query_rows, decode_key_value, decode_resid, out_weight, post_gain, prefix_page_store, prefix_table, decode_page_store, page_table, suffix_lengths, suffix_prefix, decode_ages):
    suffix_attn = suffix_part(suffix_query, suffix_key_value, prefix_page_store, prefix_table, suffix_lengths, suffix_prefix)
    decode_attn, new_cache = decode_part(decode_query_rows, decode_key_value, decode_page_store, page_table, decode_ages)
    attention = jnp.concatenate([suffix_attn, decode_attn], axis=0)
    projected = jnp.dot(attention, out_weight, preferred_element_type=jnp.float32)
    mean_square = lax.optimization_barrier(jnp.mean(projected * projected, axis=1, keepdims=True))
    normed = projected * lax.rsqrt(mean_square + norm_eps) * post_gain.astype(jnp.float32)[None, :]
    residual = jnp.concatenate([suffix_resid, decode_resid], axis=0).astype(jnp.float32)
    hidden = (residual + normed).astype(jnp.bfloat16)
    return (hidden[:SUFFIX_TOKENS], hidden[SUFFIX_TOKENS:], new_cache)
```

```python
import math

import jax
import jax.numpy as jnp
from jax import lax
from jax.sharding import PartitionSpec as P

D = 4608
QUERY_HEADS = 32
HEAD_SIZE = 128
PAGE_TOKENS = 128
PREFIX_LENGTH = 3072
SLOT_CAPACITY = 1024


soft_cap = 50.0
norm_eps = 1e-06


def from_behind(block, axis, distance):
    devices = range(lax.axis_size(axis))
    route = [(i - distance, i) for i in devices if i - distance in devices]
    return lax.ppermute(block, axis, route)


def attend(query_rows, key_rows, value_rows, visible, q_scale):
    logits = (
        jnp.einsum("qhgd,khd->qhgk", query_rows, key_rows, preferred_element_type=jnp.float32)
        * q_scale
    )
    capped = soft_cap * jnp.tanh(logits / soft_cap)
    weights = jnp.where(visible, jnp.exp(capped), 0.0)
    denominator = jnp.sum(weights, axis=3)
    numerator = jnp.einsum(
        "qhgk,khd->qhgd",
        weights.astype(jnp.bfloat16),
        value_rows,
        preferred_element_type=jnp.float32,
    )
    return (numerator, denominator)


def token_tables(lengths, prefix_ids, token_ids):
    suffix_ends = jnp.cumsum(lengths)
    starts = suffix_ends - lengths
    inside = (
        (token_ids[:, None] >= starts[None, :]) & (token_ids[:, None] < suffix_ends[None, :])
    ).astype(jnp.int32)
    tok_start = jnp.sum(inside * starts[None, :], axis=1)
    tok_prefix = jnp.sum(inside * prefix_ids[None, :], axis=1)
    return (tok_start, tok_prefix)


def inverse_rows(table, wanted):
    hits = (table[None, :] == wanted[:, None]).astype(jnp.int32)
    places = jnp.arange(table.shape[0], dtype=jnp.int32)
    return jnp.sum(hits * places[None, :], axis=1)


def body(
    suffix_query,
    suffix_key_value,
    suffix_resid,
    decode_query_rows,
    decode_key_value,
    decode_resid,
    out_weight,
    post_gain,
    prefix_page_store,
    prefix_table,
    decode_page_store,
    page_table,
    suffix_lengths,
    suffix_prefix,
    decode_ages,
):
    head_dim = HEAD_SIZE
    page_len = PAGE_TOKENS
    q_scale = (D // QUERY_HEADS) ** (-0.5)
    tok_rows = suffix_query.shape[0]
    q_heads = suffix_query.shape[1] // head_dim
    kv_heads = suffix_key_value.shape[2] // head_dim
    query_group_width = q_heads // kv_heads
    blk_size = lax.axis_size("blk")
    my_index = lax.axis_index("blk")

    local_pages = prefix_page_store.shape[1]
    dq_rows = decode_query_rows.shape[0]
    pieces = [
        prefix_page_store.reshape(-1),
        decode_query_rows.reshape(-1),
        decode_key_value.reshape(-1),
    ]
    sizes = [piece.shape[0] for piece in pieces]
    packed = jnp.concatenate(pieces)
    gathered = lax.all_gather(packed, "blk", axis=0, tiled=False)
    cut_a = sizes[0]
    cut_b = cut_a + sizes[1]
    pre_all = gathered[:, :cut_a].reshape(blk_size, 2, local_pages, page_len, kv_heads, head_dim)
    all_dq = gathered[:, cut_a:cut_b].reshape(blk_size * dq_rows, q_heads * head_dim)
    all_dkv = (
        gathered[:, cut_b:]
        .reshape(blk_size, 2, dq_rows, kv_heads * head_dim)
        .transpose(1, 0, 2, 3)
        .reshape(2, blk_size * dq_rows, kv_heads * head_dim)
    )

    look_back = 4
    pieces_back = [from_behind(suffix_key_value, "blk", d) for d in range(look_back, 0, -1)]
    window = jnp.concatenate(pieces_back + [suffix_key_value], axis=1)

    own_queries = suffix_query.reshape(tok_rows, kv_heads, query_group_width, head_dim)
    token_ids = my_index * tok_rows + jnp.arange(tok_rows, dtype=jnp.int32)
    tok_start, tok_prefix = token_tables(suffix_lengths, suffix_prefix, token_ids)
    key_ids = (my_index - look_back) * tok_rows + jnp.arange(
        (look_back + 1) * tok_rows, dtype=jnp.int32
    )
    visible = (key_ids[None, :] >= tok_start[:, None]) & (key_ids[None, :] <= token_ids[:, None])
    window_keys = window[0].reshape((look_back + 1) * tok_rows, kv_heads, head_dim)
    window_values = window[1].reshape((look_back + 1) * tok_rows, kv_heads, head_dim)
    own_numer, own_denom = attend(
        own_queries, window_keys, window_values, visible[:, None, None, :], q_scale
    )

    pool_pages = prefix_table.shape[0]
    per_prefix = PREFIX_LENGTH // PAGE_TOKENS
    page_owner = inverse_rows(prefix_table, jnp.arange(pool_pages, dtype=jnp.int32)) // per_prefix
    owner_grid = page_owner.reshape(blk_size, local_pages)
    pre_numer = jnp.zeros((tok_rows, kv_heads, query_group_width, head_dim), jnp.float32)
    pre_denom = jnp.zeros((tok_rows, kv_heads, query_group_width), jnp.float32)
    for page in range(local_pages):
        keys = pre_all[:, 0, page].reshape(blk_size * page_len, kv_heads, head_dim)
        values = pre_all[:, 1, page].reshape(blk_size * page_len, kv_heads, head_dim)
        cols = jnp.repeat(owner_grid[:, page], page_len)
        seen = tok_prefix[:, None] == cols[None, :]
        numer_c, denom_c = attend(own_queries, keys, values, seen[:, None, None, :], q_scale)
        pre_numer = pre_numer + numer_c
        pre_denom = pre_denom + denom_c
    suffix_attn = ((own_numer + pre_numer) / (own_denom + pre_denom)[..., None]).astype(
        jnp.bfloat16
    )
    suffix_attn = suffix_attn.reshape(tok_rows, q_heads * head_dim)

    slot_total = all_dq.shape[0]
    slot_pages = SLOT_CAPACITY // PAGE_TOKENS
    local_cache = decode_page_store.shape[1]
    page_ids = my_index * local_cache + jnp.arange(local_cache, dtype=jnp.int32)
    position = inverse_rows(page_table, page_ids)
    slot_of = position // slot_pages
    block_of = position % slot_pages
    slot_hot = slot_of[:, None] == jnp.arange(slot_total, dtype=jnp.int32)[None, :]
    page_age = jnp.sum(slot_hot.astype(jnp.int32) * decode_ages[None, :], axis=1)
    select = slot_hot.astype(jnp.bfloat16)
    new_rows = jnp.einsum(
        "ls,tsc->tlc", select, all_dkv, preferred_element_type=jnp.float32
    ).astype(jnp.bfloat16)
    write_here = (block_of == page_age // page_len)[:, None] & (
        jnp.arange(page_len, dtype=jnp.int32)[None, :] == (page_age % page_len)[:, None]
    )
    new_cache = jnp.where(write_here[None, :, :, None], new_rows[:, :, None, :], decode_page_store)
    page_queries = jnp.dot(select, all_dq, preferred_element_type=jnp.float32).astype(jnp.bfloat16)
    page_queries = page_queries.reshape(local_cache, kv_heads, query_group_width, head_dim)
    key_cache = new_cache[0].reshape(local_cache, page_len, kv_heads, head_dim)
    value_cache = new_cache[1].reshape(local_cache, page_len, kv_heads, head_dim)
    logits = (
        jnp.einsum("lhgd,lphd->lhgp", page_queries, key_cache, preferred_element_type=jnp.float32)
        * q_scale
    )
    capped = soft_cap * jnp.tanh(logits / soft_cap)
    places = block_of[:, None] * page_len + jnp.arange(page_len, dtype=jnp.int32)[None, :]
    seen_pos = places <= page_age[:, None]
    weights = jnp.where(seen_pos[:, None, None, :], jnp.exp(capped), 0.0)
    page_denom = jnp.sum(weights, axis=3)
    page_numer = jnp.einsum(
        "lhgp,lphd->lhgd",
        weights.astype(jnp.bfloat16),
        value_cache,
        preferred_element_type=jnp.float32,
    )
    slot_float = slot_hot.astype(jnp.float32)
    page_sums = jnp.concatenate([page_numer, page_denom[..., None]], axis=3)
    slot_sums = jnp.einsum("ls,lhgd->shgd", slot_float, page_sums, precision=lax.Precision.HIGHEST)
    mine_sums = lax.psum_scatter(slot_sums, "blk", scatter_dimension=0, tiled=True)
    mine_numer = mine_sums[..., :head_dim]
    mine_denom = mine_sums[..., head_dim]
    decode_attn = (mine_numer / mine_denom[..., None]).astype(jnp.bfloat16)
    decode_rows = decode_attn.shape[0]
    decode_attn = decode_attn.reshape(decode_rows, q_heads * head_dim)

    attention = jnp.concatenate([suffix_attn, decode_attn], axis=0)
    projected = jnp.dot(attention, out_weight, preferred_element_type=jnp.float32)
    residual = jnp.concatenate([suffix_resid, decode_resid], axis=0).astype(jnp.float32)
    mine = lax.psum_scatter(
        projected.astype(jnp.bfloat16), "kv", scatter_dimension=1, tiled=True
    ).astype(jnp.float32)
    mean_square = lax.psum(jnp.sum(mine * mine, axis=1), "kv") / D
    normed = mine * lax.rsqrt(mean_square + norm_eps)[:, None] * post_gain[None, :]
    hidden = (residual + normed).astype(jnp.bfloat16)
    return (hidden[:tok_rows], hidden[tok_rows:], new_cache)


def solution(mesh):
    placed = (
        P("blk", "kv"),
        P(None, "blk", "kv"),
        P("blk", "kv"),
        P("blk", "kv"),
        P(None, "blk", "kv"),
        P("blk", "kv"),
        P("kv", None),
        P("kv"),
        P(None, "blk", None, "kv"),
        P(),
        P(None, "blk", None, "kv"),
        P(),
        P(),
        P(),
        P(),
    )
    return jax.shard_map(
        body,
        mesh=mesh,
        in_specs=placed,
        out_specs=(P("blk", "kv"), P("blk", "kv"), P(None, "blk", None, "kv")),
        check_vma=False,
    )
```

```python
import math

import jax
import jax.numpy as jnp
from jax import lax
from jax.sharding import PartitionSpec as P

D = 4608
QUERY_HEADS = 32
HEAD_SIZE = 128
PAGE_TOKENS = 128
PREFIX_LENGTH = 3072
SLOT_CAPACITY = 1024


soft_cap = 50.0
norm_eps = 1e-06


def from_behind(block, axis, distance):
    devices = range(lax.axis_size(axis))
    route = [(i - distance, i) for i in devices if i - distance in devices]
    return lax.ppermute(block, axis, route)


def attend(query_rows, key_rows, value_rows, visible, q_scale):
    logits = (
        jnp.einsum("qhgd,khd->qhgk", query_rows, key_rows, preferred_element_type=jnp.float32)
        * q_scale
    )
    capped = soft_cap * jnp.tanh(logits / soft_cap)
    weights = jnp.where(visible, jnp.exp(capped), 0.0)
    denominator = jnp.sum(weights, axis=3)
    numerator = jnp.einsum(
        "qhgk,khd->qhgd",
        weights.astype(jnp.bfloat16),
        value_rows,
        preferred_element_type=jnp.float32,
    )
    return (numerator, denominator)


def token_tables(lengths, prefix_ids, token_ids):
    suffix_ends = jnp.cumsum(lengths)
    starts = suffix_ends - lengths
    inside = (
        (token_ids[:, None] >= starts[None, :]) & (token_ids[:, None] < suffix_ends[None, :])
    ).astype(jnp.int32)
    tok_start = jnp.sum(inside * starts[None, :], axis=1)
    tok_prefix = jnp.sum(inside * prefix_ids[None, :], axis=1)
    return (tok_start, tok_prefix)


def inverse_rows(table, wanted):
    hits = (table[None, :] == wanted[:, None]).astype(jnp.int32)
    places = jnp.arange(table.shape[0], dtype=jnp.int32)
    return jnp.sum(hits * places[None, :], axis=1)


def body(
    suffix_query,
    suffix_key_value,
    suffix_resid,
    decode_query_rows,
    decode_key_value,
    decode_resid,
    out_weight,
    post_gain,
    prefix_page_store,
    prefix_table,
    decode_page_store,
    page_table,
    suffix_lengths,
    suffix_prefix,
    decode_ages,
):
    head_dim = HEAD_SIZE
    page_len = PAGE_TOKENS
    q_scale = (D // QUERY_HEADS) ** (-0.5)
    tok_rows = suffix_query.shape[0]
    q_heads = suffix_query.shape[1] // head_dim
    kv_heads = suffix_key_value.shape[2] // head_dim
    query_group_width = q_heads // kv_heads
    blk_size = lax.axis_size("blk")
    my_index = lax.axis_index("blk")

    local_pages = prefix_page_store.shape[1]
    dq_rows = decode_query_rows.shape[0]
    kv_width = kv_heads * head_dim
    held_rows = local_pages * page_len
    dq_lines = decode_query_rows.size // kv_width
    dkv_lines = decode_key_value.size // kv_width
    extra_lines = 16
    extra = jnp.zeros((2, extra_lines, kv_width), jnp.bfloat16)
    extra = extra.at[0, :dq_lines].set(decode_query_rows.reshape(dq_lines, kv_width))
    extra = extra.at[1, :dkv_lines].set(decode_key_value.reshape(dkv_lines, kv_width))
    packed = jnp.concatenate([prefix_page_store.reshape(2, held_rows, kv_width), extra], axis=1)
    gathered = lax.all_gather(packed, "blk", axis=0, tiled=False)
    all_keys = gathered[:, 0, :held_rows].reshape(blk_size * held_rows, kv_heads, head_dim)
    all_values = gathered[:, 1, :held_rows].reshape(blk_size * held_rows, kv_heads, head_dim)
    all_dq = gathered[:, 0, held_rows : held_rows + dq_lines].reshape(
        blk_size * dq_rows, q_heads * head_dim
    )
    all_dkv = (
        gathered[:, 1, held_rows : held_rows + dkv_lines]
        .reshape(blk_size, 2, dq_rows, kv_width)
        .transpose(1, 0, 2, 3)
        .reshape(2, blk_size * dq_rows, kv_width)
    )

    look_back = 4
    pieces_back = [from_behind(suffix_key_value, "blk", d) for d in range(look_back, 0, -1)]
    window = jnp.concatenate(pieces_back + [suffix_key_value], axis=1)

    own_queries = suffix_query.reshape(tok_rows, kv_heads, query_group_width, head_dim)
    token_ids = my_index * tok_rows + jnp.arange(tok_rows, dtype=jnp.int32)
    tok_start, tok_prefix = token_tables(suffix_lengths, suffix_prefix, token_ids)
    key_ids = (my_index - look_back) * tok_rows + jnp.arange(
        (look_back + 1) * tok_rows, dtype=jnp.int32
    )
    visible = (key_ids[None, :] >= tok_start[:, None]) & (key_ids[None, :] <= token_ids[:, None])
    window_keys = window[0].reshape((look_back + 1) * tok_rows, kv_heads, head_dim)
    window_values = window[1].reshape((look_back + 1) * tok_rows, kv_heads, head_dim)
    own_numer, own_denom = attend(
        own_queries, window_keys, window_values, visible[:, None, None, :], q_scale
    )

    pool_pages = prefix_table.shape[0]
    per_prefix = PREFIX_LENGTH // PAGE_TOKENS
    page_owner = inverse_rows(prefix_table, jnp.arange(pool_pages, dtype=jnp.int32)) // per_prefix
    key_owner = jnp.repeat(page_owner, page_len)
    pre_numer = jnp.zeros((tok_rows, kv_heads, query_group_width, head_dim), jnp.float32)
    pre_denom = jnp.zeros((tok_rows, kv_heads, query_group_width), jnp.float32)
    chunks = 3
    chunk_keys = all_keys.shape[0] // chunks
    for chunk in range(chunks):
        span = slice(chunk * chunk_keys, (chunk + 1) * chunk_keys)
        seen = tok_prefix[:, None] == key_owner[span][None, :]
        numer_c, denom_c = attend(
            own_queries, all_keys[span], all_values[span], seen[:, None, None, :], q_scale
        )
        pre_numer = pre_numer + numer_c
        pre_denom = pre_denom + denom_c
    suffix_attn = ((own_numer + pre_numer) / (own_denom + pre_denom)[..., None]).astype(
        jnp.bfloat16
    )
    suffix_attn = suffix_attn.reshape(tok_rows, q_heads * head_dim)

    slot_total = all_dq.shape[0]
    slot_pages = SLOT_CAPACITY // PAGE_TOKENS
    local_cache = decode_page_store.shape[1]
    page_ids = my_index * local_cache + jnp.arange(local_cache, dtype=jnp.int32)
    position = inverse_rows(page_table, page_ids)
    slot_of = position // slot_pages
    block_of = position % slot_pages
    slot_hot = slot_of[:, None] == jnp.arange(slot_total, dtype=jnp.int32)[None, :]
    page_age = jnp.sum(slot_hot.astype(jnp.int32) * decode_ages[None, :], axis=1)
    select = slot_hot.astype(jnp.bfloat16)
    new_rows = jnp.einsum(
        "ls,tsc->tlc", select, all_dkv, preferred_element_type=jnp.float32
    ).astype(jnp.bfloat16)
    write_here = (block_of == page_age // page_len)[:, None] & (
        jnp.arange(page_len, dtype=jnp.int32)[None, :] == (page_age % page_len)[:, None]
    )
    new_cache = jnp.where(write_here[None, :, :, None], new_rows[:, :, None, :], decode_page_store)
    page_queries = jnp.dot(select, all_dq, preferred_element_type=jnp.float32).astype(jnp.bfloat16)
    page_queries = page_queries.reshape(local_cache, kv_heads, query_group_width, head_dim)
    key_cache = new_cache[0].reshape(local_cache, page_len, kv_heads, head_dim)
    value_cache = new_cache[1].reshape(local_cache, page_len, kv_heads, head_dim)
    logits = (
        jnp.einsum("lhgd,lphd->lhgp", page_queries, key_cache, preferred_element_type=jnp.float32)
        * q_scale
    )
    capped = soft_cap * jnp.tanh(logits / soft_cap)
    places = block_of[:, None] * page_len + jnp.arange(page_len, dtype=jnp.int32)[None, :]
    seen_pos = places <= page_age[:, None]
    weights = jnp.where(seen_pos[:, None, None, :], jnp.exp(capped), 0.0)
    page_denom = jnp.sum(weights, axis=3)
    page_numer = jnp.einsum(
        "lhgp,lphd->lhgd",
        weights.astype(jnp.bfloat16),
        value_cache,
        preferred_element_type=jnp.float32,
    )
    slot_float = slot_hot.astype(jnp.float32)
    page_sums = jnp.concatenate([page_numer, page_denom[..., None]], axis=3)
    slot_sums = jnp.einsum("ls,lhgd->shgd", slot_float, page_sums, precision=lax.Precision.HIGHEST)
    slot_sums = slot_sums.reshape((blk_size, slot_total // blk_size) + slot_sums.shape[1:])
    mine_sums = jnp.sum(lax.all_to_all(slot_sums, "blk", 0, 0, tiled=False), axis=0)
    mine_numer = mine_sums[..., :head_dim]
    mine_denom = mine_sums[..., head_dim]
    decode_attn = (mine_numer / mine_denom[..., None]).astype(jnp.bfloat16)
    decode_rows = decode_attn.shape[0]
    decode_attn = decode_attn.reshape(decode_rows, q_heads * head_dim)

    attention = jnp.concatenate([suffix_attn, decode_attn], axis=0)
    projected = jnp.dot(attention, out_weight, preferred_element_type=jnp.float32)
    residual = jnp.concatenate([suffix_resid, decode_resid], axis=0).astype(jnp.float32)
    kv_size = lax.axis_size("kv")
    shares = projected.astype(jnp.bfloat16).reshape(projected.shape[0], kv_size, -1)
    mine = jnp.sum(
        lax.all_to_all(shares, "kv", 1, 1, tiled=False).astype(jnp.float32), axis=1
    )
    mean_square = lax.psum(jnp.sum(mine * mine, axis=1), "kv") / D
    normed = mine * lax.rsqrt(mean_square + norm_eps)[:, None] * post_gain[None, :]
    hidden = (residual + normed).astype(jnp.bfloat16)
    return (hidden[:tok_rows], hidden[tok_rows:], new_cache)


def solution(mesh):
    placed = (
        P("blk", "kv"),
        P(None, "blk", "kv"),
        P("blk", "kv"),
        P("blk", "kv"),
        P(None, "blk", "kv"),
        P("blk", "kv"),
        P("kv", None),
        P("kv"),
        P(None, "blk", None, "kv"),
        P(),
        P(None, "blk", None, "kv"),
        P(),
        P(),
        P(),
        P(),
    )
    return jax.shard_map(
        body,
        mesh=mesh,
        in_specs=placed,
        out_specs=(P("blk", "kv"), P("blk", "kv"), P(None, "blk", None, "kv")),
        check_vma=False,
    )
```

```python
import math

import jax
import jax.numpy as jnp
from jax import lax
from jax.sharding import PartitionSpec as P

D = 4608
QUERY_HEADS = 32
HEAD_SIZE = 128
PAGE_TOKENS = 128
PREFIX_LENGTH = 3072
SLOT_CAPACITY = 1024


soft_cap = 50.0
norm_eps = 1e-06


def from_behind(block, axis, distance):
    devices = range(lax.axis_size(axis))
    route = [(i - distance, i) for i in devices if i - distance in devices]
    return lax.ppermute(block, axis, route)


def attend(query_rows, key_rows, value_rows, visible, q_scale):
    logits = (
        jnp.einsum("qhgd,khd->qhgk", query_rows, key_rows, preferred_element_type=jnp.float32)
        * q_scale
    )
    capped = soft_cap * jnp.tanh(logits / soft_cap)
    weights = jnp.where(visible, jnp.exp(capped), 0.0)
    denominator = jnp.sum(weights, axis=3)
    numerator = jnp.einsum(
        "qhgk,khd->qhgd",
        weights.astype(jnp.bfloat16),
        value_rows,
        preferred_element_type=jnp.float32,
    )
    return (numerator, denominator)


def attend_rows(query_rows, key_rows, value_rows, visible, q_scale):
    logits = (
        jnp.dot(query_rows, key_rows.T, preferred_element_type=jnp.float32) * q_scale
    )
    capped = soft_cap * jnp.tanh(logits / soft_cap)
    weights = jnp.where(visible, jnp.exp(capped), 0.0)
    denominator = jnp.sum(weights, axis=1)
    numerator = jnp.dot(
        weights.astype(jnp.bfloat16), value_rows, preferred_element_type=jnp.float32
    )
    return (numerator, denominator)


def token_tables(lengths, prefix_ids, token_ids):
    suffix_ends = jnp.cumsum(lengths)
    starts = suffix_ends - lengths
    inside = (
        (token_ids[:, None] >= starts[None, :]) & (token_ids[:, None] < suffix_ends[None, :])
    ).astype(jnp.int32)
    tok_start = jnp.sum(inside * starts[None, :], axis=1)
    tok_prefix = jnp.sum(inside * prefix_ids[None, :], axis=1)
    return (tok_start, tok_prefix)


def inverse_rows(table, wanted):
    hits = (table[None, :] == wanted[:, None]).astype(jnp.int32)
    places = jnp.arange(table.shape[0], dtype=jnp.int32)
    return jnp.sum(hits * places[None, :], axis=1)


def body(
    suffix_query,
    suffix_key_value,
    suffix_resid,
    decode_query_rows,
    decode_key_value,
    decode_resid,
    out_weight,
    post_gain,
    prefix_page_store,
    prefix_table,
    decode_page_store,
    page_table,
    suffix_lengths,
    suffix_prefix,
    decode_ages,
):
    head_dim = HEAD_SIZE
    page_len = PAGE_TOKENS
    q_scale = (D // QUERY_HEADS) ** (-0.5)
    tok_rows = suffix_query.shape[0]
    q_heads = suffix_query.shape[1] // head_dim
    kv_heads = suffix_key_value.shape[2] // head_dim
    query_group_width = q_heads // kv_heads
    blk_size = lax.axis_size("blk")
    my_index = lax.axis_index("blk")

    local_pages = prefix_page_store.shape[1]
    dq_rows = decode_query_rows.shape[0]
    kv_width = kv_heads * head_dim
    held_rows = local_pages * page_len
    dq_lines = decode_query_rows.size // kv_width
    dkv_lines = decode_key_value.size // kv_width
    extra_lines = 16
    extra = jnp.zeros((2, extra_lines, kv_width), jnp.bfloat16)
    extra = extra.at[0, :dq_lines].set(decode_query_rows.reshape(dq_lines, kv_width))
    extra = extra.at[1, :dkv_lines].set(decode_key_value.reshape(dkv_lines, kv_width))
    packed = jnp.concatenate([prefix_page_store.reshape(2, held_rows, kv_width), extra], axis=1)
    gathered = lax.all_gather(packed, "blk", axis=0, tiled=False)
    all_dq = gathered[:, 0, held_rows : held_rows + dq_lines].reshape(
        blk_size * dq_rows, q_heads * head_dim
    )
    all_dkv = (
        gathered[:, 1, held_rows : held_rows + dkv_lines]
        .reshape(blk_size, 2, dq_rows, kv_width)
        .transpose(1, 0, 2, 3)
        .reshape(2, blk_size * dq_rows, kv_width)
    )

    look_back = 4
    pieces_back = [from_behind(suffix_key_value, "blk", d) for d in range(look_back, 0, -1)]
    window = jnp.concatenate(pieces_back + [suffix_key_value], axis=1)

    own_queries = suffix_query.reshape(tok_rows, kv_heads, query_group_width, head_dim)
    token_ids = my_index * tok_rows + jnp.arange(tok_rows, dtype=jnp.int32)
    tok_start, tok_prefix = token_tables(suffix_lengths, suffix_prefix, token_ids)
    key_ids = (my_index - look_back) * tok_rows + jnp.arange(
        (look_back + 1) * tok_rows, dtype=jnp.int32
    )
    visible = (key_ids[None, :] >= tok_start[:, None]) & (key_ids[None, :] <= token_ids[:, None])
    window_keys = window[0].reshape((look_back + 1) * tok_rows, kv_heads, head_dim)
    window_values = window[1].reshape((look_back + 1) * tok_rows, kv_heads, head_dim)
    own_numer, own_denom = attend(
        own_queries, window_keys, window_values, visible[:, None, None, :], q_scale
    )

    pool_pages = prefix_table.shape[0]
    per_prefix = PREFIX_LENGTH // PAGE_TOKENS
    page_owner = inverse_rows(prefix_table, jnp.arange(pool_pages, dtype=jnp.int32)) // per_prefix
    key_owner = jnp.repeat(page_owner, page_len)
    row_prefix = jnp.repeat(tok_prefix, query_group_width)
    chunks = 3
    chunk_keys = blk_size * held_rows // chunks
    head_numer = []
    head_denom = []
    for head in range(kv_heads):
        lanes = slice(head * head_dim, (head + 1) * head_dim)
        head_keys = gathered[:, 0, :held_rows, lanes].reshape(blk_size * held_rows, head_dim)
        head_values = gathered[:, 1, :held_rows, lanes].reshape(blk_size * held_rows, head_dim)
        head_queries = own_queries[:, head].reshape(tok_rows * query_group_width, head_dim)
        numer_h = jnp.zeros((tok_rows * query_group_width, head_dim), jnp.float32)
        denom_h = jnp.zeros((tok_rows * query_group_width,), jnp.float32)
        for chunk in range(chunks):
            span = slice(chunk * chunk_keys, (chunk + 1) * chunk_keys)
            seen = row_prefix[:, None] == key_owner[span][None, :]
            numer_c, denom_c = attend_rows(
                head_queries, head_keys[span], head_values[span], seen, q_scale
            )
            numer_h = numer_h + numer_c
            denom_h = denom_h + denom_c
        head_numer.append(numer_h.reshape(tok_rows, query_group_width, head_dim))
        head_denom.append(denom_h.reshape(tok_rows, query_group_width))
    pre_numer = jnp.stack(head_numer, axis=1)
    pre_denom = jnp.stack(head_denom, axis=1)
    suffix_attn = ((own_numer + pre_numer) / (own_denom + pre_denom)[..., None]).astype(
        jnp.bfloat16
    )
    suffix_attn = suffix_attn.reshape(tok_rows, q_heads * head_dim)

    slot_total = all_dq.shape[0]
    slot_pages = SLOT_CAPACITY // PAGE_TOKENS
    local_cache = decode_page_store.shape[1]
    page_ids = my_index * local_cache + jnp.arange(local_cache, dtype=jnp.int32)
    position = inverse_rows(page_table, page_ids)
    slot_of = position // slot_pages
    block_of = position % slot_pages
    slot_hot = slot_of[:, None] == jnp.arange(slot_total, dtype=jnp.int32)[None, :]
    page_age = jnp.sum(slot_hot.astype(jnp.int32) * decode_ages[None, :], axis=1)
    select = slot_hot.astype(jnp.bfloat16)
    new_rows = jnp.einsum(
        "ls,tsc->tlc", select, all_dkv, preferred_element_type=jnp.float32
    ).astype(jnp.bfloat16)
    write_here = (block_of == page_age // page_len)[:, None] & (
        jnp.arange(page_len, dtype=jnp.int32)[None, :] == (page_age % page_len)[:, None]
    )
    new_cache = jnp.where(write_here[None, :, :, None], new_rows[:, :, None, :], decode_page_store)
    page_queries = jnp.dot(select, all_dq, preferred_element_type=jnp.float32).astype(jnp.bfloat16)
    page_queries = page_queries.reshape(local_cache, kv_heads, query_group_width, head_dim)
    key_cache = new_cache[0].reshape(local_cache, page_len, kv_heads, head_dim)
    value_cache = new_cache[1].reshape(local_cache, page_len, kv_heads, head_dim)
    logits = (
        jnp.einsum("lhgd,lphd->lhgp", page_queries, key_cache, preferred_element_type=jnp.float32)
        * q_scale
    )
    capped = soft_cap * jnp.tanh(logits / soft_cap)
    places = block_of[:, None] * page_len + jnp.arange(page_len, dtype=jnp.int32)[None, :]
    seen_pos = places <= page_age[:, None]
    weights = jnp.where(seen_pos[:, None, None, :], jnp.exp(capped), 0.0)
    page_denom = jnp.sum(weights, axis=3)
    page_numer = jnp.einsum(
        "lhgp,lphd->lhgd",
        weights.astype(jnp.bfloat16),
        value_cache,
        preferred_element_type=jnp.float32,
    )
    slot_float = slot_hot.astype(jnp.float32)
    page_sums = jnp.concatenate([page_numer, page_denom[..., None]], axis=3)
    slot_sums = jnp.einsum("ls,lhgd->shgd", slot_float, page_sums, precision=lax.Precision.HIGHEST)
    slot_sums = slot_sums.reshape((blk_size, slot_total // blk_size) + slot_sums.shape[1:])
    mine_sums = jnp.sum(lax.all_to_all(slot_sums, "blk", 0, 0, tiled=False), axis=0)
    mine_numer = mine_sums[..., :head_dim]
    mine_denom = mine_sums[..., head_dim]
    decode_attn = (mine_numer / mine_denom[..., None]).astype(jnp.bfloat16)
    decode_rows = decode_attn.shape[0]
    decode_attn = decode_attn.reshape(decode_rows, q_heads * head_dim)

    attention = jnp.concatenate([suffix_attn, decode_attn], axis=0)
    projected = jnp.dot(attention, out_weight, preferred_element_type=jnp.float32)
    residual = jnp.concatenate([suffix_resid, decode_resid], axis=0).astype(jnp.float32)
    kv_size = lax.axis_size("kv")
    shares = projected.astype(jnp.bfloat16).reshape(projected.shape[0], kv_size, -1)
    mine = jnp.sum(
        lax.all_to_all(shares, "kv", 1, 1, tiled=False).astype(jnp.float32), axis=1
    )
    mean_square = lax.psum(jnp.sum(mine * mine, axis=1), "kv") / D
    normed = mine * lax.rsqrt(mean_square + norm_eps)[:, None] * post_gain[None, :]
    hidden = (residual + normed).astype(jnp.bfloat16)
    return (hidden[:tok_rows], hidden[tok_rows:], new_cache)


def solution(mesh):
    placed = (
        P("blk", "kv"),
        P(None, "blk", "kv"),
        P("blk", "kv"),
        P("blk", "kv"),
        P(None, "blk", "kv"),
        P("blk", "kv"),
        P("kv", None),
        P("kv"),
        P(None, "blk", None, "kv"),
        P(),
        P(None, "blk", None, "kv"),
        P(),
        P(),
        P(),
        P(),
    )
    return jax.shard_map(
        body,
        mesh=mesh,
        in_specs=placed,
        out_specs=(P("blk", "kv"), P("blk", "kv"), P(None, "blk", None, "kv")),
        check_vma=False,
    )
```

```python
import math

import jax
import jax.numpy as jnp
from jax import lax
from jax.sharding import PartitionSpec as P

D = 4608
QUERY_HEADS = 32
HEAD_SIZE = 128
PAGE_TOKENS = 128
PREFIX_LENGTH = 3072
SLOT_CAPACITY = 1024


soft_cap = 50.0
norm_eps = 1e-06


def from_behind(block, axis, distance):
    devices = range(lax.axis_size(axis))
    route = [(i - distance, i) for i in devices if i - distance in devices]
    return lax.ppermute(block, axis, route)


def attend(query_rows, key_rows, value_rows, visible, q_scale):
    logits = (
        jnp.einsum("qhgd,khd->qhgk", query_rows, key_rows, preferred_element_type=jnp.float32)
        * q_scale
    )
    capped = soft_cap * jnp.tanh(logits / soft_cap)
    weights = jnp.where(visible, jnp.exp(capped), 0.0)
    denominator = jnp.sum(weights, axis=3)
    numerator = jnp.einsum(
        "qhgk,khd->qhgd",
        weights.astype(jnp.bfloat16),
        value_rows,
        preferred_element_type=jnp.float32,
    )
    return (numerator, denominator)


def attend_rows(query_rows, key_rows, value_rows, visible, q_scale):
    logits = (
        jnp.dot(query_rows, key_rows.T, preferred_element_type=jnp.float32) * q_scale
    )
    capped = soft_cap * jnp.tanh(logits / soft_cap)
    weights = jnp.where(visible, jnp.exp(capped), 0.0)
    denominator = jnp.sum(weights, axis=1)
    numerator = jnp.dot(
        weights.astype(jnp.bfloat16), value_rows, preferred_element_type=jnp.float32
    )
    return (numerator, denominator)


def token_tables(lengths, prefix_ids, token_ids):
    suffix_ends = jnp.cumsum(lengths)
    starts = suffix_ends - lengths
    inside = (
        (token_ids[:, None] >= starts[None, :]) & (token_ids[:, None] < suffix_ends[None, :])
    ).astype(jnp.int32)
    tok_start = jnp.sum(inside * starts[None, :], axis=1)
    tok_prefix = jnp.sum(inside * prefix_ids[None, :], axis=1)
    return (tok_start, tok_prefix)


def inverse_rows(table, wanted):
    hits = (table[None, :] == wanted[:, None]).astype(jnp.int32)
    places = jnp.arange(table.shape[0], dtype=jnp.int32)
    return jnp.sum(hits * places[None, :], axis=1)


def body(
    suffix_query,
    suffix_key_value,
    suffix_resid,
    decode_query_rows,
    decode_key_value,
    decode_resid,
    out_weight,
    post_gain,
    prefix_page_store,
    prefix_table,
    decode_page_store,
    page_table,
    suffix_lengths,
    suffix_prefix,
    decode_ages,
):
    head_dim = HEAD_SIZE
    page_len = PAGE_TOKENS
    q_scale = (D // QUERY_HEADS) ** (-0.5)
    tok_rows = suffix_query.shape[0]
    q_heads = suffix_query.shape[1] // head_dim
    kv_heads = suffix_key_value.shape[2] // head_dim
    query_group_width = q_heads // kv_heads
    blk_size = lax.axis_size("blk")
    my_index = lax.axis_index("blk")

    local_pages = prefix_page_store.shape[1]
    dq_rows = decode_query_rows.shape[0]
    kv_width = kv_heads * head_dim
    dq_lines = decode_query_rows.size // kv_width
    dkv_lines = decode_key_value.size // kv_width
    dec_local = jnp.concatenate(
        [
            decode_query_rows.reshape(dq_lines, kv_width),
            decode_key_value.reshape(dkv_lines, kv_width),
        ],
        axis=0,
    )
    dec_all = lax.all_to_all(
        jnp.broadcast_to(dec_local[None], (blk_size,) + dec_local.shape), "blk", 0, 0, tiled=False
    )
    all_dq = dec_all[:, :dq_lines].reshape(blk_size * dq_rows, q_heads * head_dim)
    all_dkv = (
        dec_all[:, dq_lines:]
        .reshape(blk_size, 2, dq_rows, kv_width)
        .transpose(1, 0, 2, 3)
        .reshape(2, blk_size * dq_rows, kv_width)
    )

    gathered_pages = []
    for page in range(local_pages):
        piece = (
            prefix_page_store[:, page]
            .reshape(2, page_len, kv_heads, head_dim)
            .transpose(0, 2, 1, 3)
        )
        gathered_pages.append(lax.all_gather(piece, "blk", axis=0, tiled=False))

    look_back = 4
    pieces_back = [from_behind(suffix_key_value, "blk", d) for d in range(look_back, 0, -1)]
    window = jnp.concatenate(pieces_back + [suffix_key_value], axis=1)

    own_queries = suffix_query.reshape(tok_rows, kv_heads, query_group_width, head_dim)
    token_ids = my_index * tok_rows + jnp.arange(tok_rows, dtype=jnp.int32)
    tok_start, tok_prefix = token_tables(suffix_lengths, suffix_prefix, token_ids)
    key_ids = (my_index - look_back) * tok_rows + jnp.arange(
        (look_back + 1) * tok_rows, dtype=jnp.int32
    )
    visible = (key_ids[None, :] >= tok_start[:, None]) & (key_ids[None, :] <= token_ids[:, None])
    window_keys = window[0].reshape((look_back + 1) * tok_rows, kv_heads, head_dim)
    window_values = window[1].reshape((look_back + 1) * tok_rows, kv_heads, head_dim)
    own_numer, own_denom = attend(
        own_queries, window_keys, window_values, visible[:, None, None, :], q_scale
    )

    pool_pages = prefix_table.shape[0]
    per_prefix = PREFIX_LENGTH // PAGE_TOKENS
    page_owner = inverse_rows(prefix_table, jnp.arange(pool_pages, dtype=jnp.int32)) // per_prefix
    owner_grid = page_owner.reshape(blk_size, local_pages)
    row_prefix = jnp.repeat(tok_prefix, query_group_width)
    rows_q = tok_rows * query_group_width
    sums = [
        (jnp.zeros((rows_q, head_dim), jnp.float32), jnp.zeros((rows_q,), jnp.float32))
        for head in range(kv_heads)
    ]
    for page in range(local_pages):
        page_block = gathered_pages[page]
        if page > 0:
            sums, page_block = lax.optimization_barrier((sums, page_block))
        key_owner = jnp.repeat(owner_grid[:, page], page_len)
        seen = row_prefix[:, None] == key_owner[None, :]
        for head in range(kv_heads):
            head_queries = own_queries[:, head].reshape(rows_q, head_dim)
            head_keys = page_block[:, 0, head].reshape(blk_size * page_len, head_dim)
            head_values = page_block[:, 1, head].reshape(blk_size * page_len, head_dim)
            numer_c, denom_c = attend_rows(head_queries, head_keys, head_values, seen, q_scale)
            sums[head] = (sums[head][0] + numer_c, sums[head][1] + denom_c)
    head_numer = [numer.reshape(tok_rows, query_group_width, head_dim) for numer, _ in sums]
    head_denom = [denom.reshape(tok_rows, query_group_width) for _, denom in sums]
    pre_numer = jnp.stack(head_numer, axis=1)
    pre_denom = jnp.stack(head_denom, axis=1)
    suffix_attn = ((own_numer + pre_numer) / (own_denom + pre_denom)[..., None]).astype(
        jnp.bfloat16
    )
    suffix_attn = suffix_attn.reshape(tok_rows, q_heads * head_dim)

    slot_total = all_dq.shape[0]
    slot_pages = SLOT_CAPACITY // PAGE_TOKENS
    local_cache = decode_page_store.shape[1]
    page_ids = my_index * local_cache + jnp.arange(local_cache, dtype=jnp.int32)
    position = inverse_rows(page_table, page_ids)
    slot_of = position // slot_pages
    block_of = position % slot_pages
    slot_hot = slot_of[:, None] == jnp.arange(slot_total, dtype=jnp.int32)[None, :]
    page_age = jnp.sum(slot_hot.astype(jnp.int32) * decode_ages[None, :], axis=1)
    select = slot_hot.astype(jnp.bfloat16)
    new_rows = jnp.einsum(
        "ls,tsc->tlc", select, all_dkv, preferred_element_type=jnp.float32
    ).astype(jnp.bfloat16)
    write_here = (block_of == page_age // page_len)[:, None] & (
        jnp.arange(page_len, dtype=jnp.int32)[None, :] == (page_age % page_len)[:, None]
    )
    new_cache = jnp.where(write_here[None, :, :, None], new_rows[:, :, None, :], decode_page_store)
    page_queries = jnp.dot(select, all_dq, preferred_element_type=jnp.float32).astype(jnp.bfloat16)
    page_queries = page_queries.reshape(local_cache, kv_heads, query_group_width, head_dim)
    key_cache = new_cache[0].reshape(local_cache, page_len, kv_heads, head_dim)
    value_cache = new_cache[1].reshape(local_cache, page_len, kv_heads, head_dim)
    logits = (
        jnp.einsum("lhgd,lphd->lhgp", page_queries, key_cache, preferred_element_type=jnp.float32)
        * q_scale
    )
    capped = soft_cap * jnp.tanh(logits / soft_cap)
    places = block_of[:, None] * page_len + jnp.arange(page_len, dtype=jnp.int32)[None, :]
    seen_pos = places <= page_age[:, None]
    weights = jnp.where(seen_pos[:, None, None, :], jnp.exp(capped), 0.0)
    page_denom = jnp.sum(weights, axis=3)
    page_numer = jnp.einsum(
        "lhgp,lphd->lhgd",
        weights.astype(jnp.bfloat16),
        value_cache,
        preferred_element_type=jnp.float32,
    )
    slot_float = slot_hot.astype(jnp.float32)
    page_sums = jnp.concatenate([page_numer, page_denom[..., None]], axis=3)
    slot_sums = jnp.einsum("ls,lhgd->shgd", slot_float, page_sums, precision=lax.Precision.HIGHEST)
    slot_sums = slot_sums.reshape((blk_size, slot_total // blk_size) + slot_sums.shape[1:])
    mine_sums = jnp.sum(lax.all_to_all(slot_sums, "blk", 0, 0, tiled=False), axis=0)
    mine_numer = mine_sums[..., :head_dim]
    mine_denom = mine_sums[..., head_dim]
    decode_attn = (mine_numer / mine_denom[..., None]).astype(jnp.bfloat16)
    decode_rows = decode_attn.shape[0]
    decode_attn = decode_attn.reshape(decode_rows, q_heads * head_dim)

    attention = jnp.concatenate([suffix_attn, decode_attn], axis=0)
    projected = jnp.dot(attention, out_weight, preferred_element_type=jnp.float32)
    residual = jnp.concatenate([suffix_resid, decode_resid], axis=0).astype(jnp.float32)
    kv_size = lax.axis_size("kv")
    shares = projected.astype(jnp.bfloat16).reshape(projected.shape[0], kv_size, -1)
    mine = jnp.sum(
        lax.all_to_all(shares, "kv", 1, 1, tiled=False).astype(jnp.float32), axis=1
    )
    squares = jnp.sum(mine * mine, axis=1)
    square_parts = lax.all_to_all(
        jnp.broadcast_to(squares[None], (kv_size,) + squares.shape), "kv", 0, 0, tiled=False
    )
    mean_square = jnp.sum(square_parts, axis=0) / D
    normed = mine * lax.rsqrt(mean_square + norm_eps)[:, None] * post_gain[None, :]
    hidden = (residual + normed).astype(jnp.bfloat16)
    return (hidden[:tok_rows], hidden[tok_rows:], new_cache)


def solution(mesh):
    placed = (
        P("blk", "kv"),
        P(None, "blk", "kv"),
        P("blk", "kv"),
        P("blk", "kv"),
        P(None, "blk", "kv"),
        P("blk", "kv"),
        P("kv", None),
        P("kv"),
        P(None, "blk", None, "kv"),
        P(),
        P(None, "blk", None, "kv"),
        P(),
        P(),
        P(),
        P(),
    )
    return jax.shard_map(
        body,
        mesh=mesh,
        in_specs=placed,
        out_specs=(P("blk", "kv"), P("blk", "kv"), P(None, "blk", None, "kv")),
        check_vma=False,
    )
```

```python
import math

import jax
import jax.numpy as jnp
from jax import lax
from jax.sharding import PartitionSpec as P

D = 4608
QUERY_HEADS = 32
HEAD_SIZE = 128
PAGE_TOKENS = 128
PREFIX_LENGTH = 3072
SLOT_CAPACITY = 1024


soft_cap = 50.0
norm_eps = 1e-06


def from_behind(block, axis, distance):
    devices = range(lax.axis_size(axis))
    route = [(i - distance, i) for i in devices if i - distance in devices]
    return lax.ppermute(block, axis, route)


def attend(query_rows, key_rows, value_rows, visible, q_scale):
    logits = (
        jnp.einsum("qhgd,khd->qhgk", query_rows, key_rows, preferred_element_type=jnp.float32)
        * q_scale
    )
    capped = soft_cap * jnp.tanh(logits / soft_cap)
    weights = jnp.where(visible, jnp.exp(capped), 0.0)
    denominator = jnp.sum(weights, axis=3)
    numerator = jnp.einsum(
        "qhgk,khd->qhgd",
        weights.astype(jnp.bfloat16),
        value_rows,
        preferred_element_type=jnp.float32,
    )
    return (numerator, denominator)


def attend_rows(query_rows, key_rows, value_rows, visible, q_scale):
    logits = (
        jnp.dot(query_rows, key_rows.T, preferred_element_type=jnp.float32) * q_scale
    )
    capped = soft_cap * jnp.tanh(logits / soft_cap)
    weights = jnp.where(visible, jnp.exp(capped), 0.0)
    denominator = jnp.sum(weights, axis=1)
    numerator = jnp.dot(
        weights.astype(jnp.bfloat16), value_rows, preferred_element_type=jnp.float32
    )
    return (numerator, denominator)


def token_tables(lengths, prefix_ids, token_ids):
    suffix_ends = jnp.cumsum(lengths)
    starts = suffix_ends - lengths
    inside = (
        (token_ids[:, None] >= starts[None, :]) & (token_ids[:, None] < suffix_ends[None, :])
    ).astype(jnp.int32)
    tok_start = jnp.sum(inside * starts[None, :], axis=1)
    tok_prefix = jnp.sum(inside * prefix_ids[None, :], axis=1)
    return (tok_start, tok_prefix)


def inverse_rows(table, wanted):
    hits = (table[None, :] == wanted[:, None]).astype(jnp.int32)
    places = jnp.arange(table.shape[0], dtype=jnp.int32)
    return jnp.sum(hits * places[None, :], axis=1)


def body(
    suffix_query,
    suffix_key_value,
    suffix_resid,
    decode_query_rows,
    decode_key_value,
    decode_resid,
    out_weight,
    post_gain,
    prefix_page_store,
    prefix_table,
    decode_page_store,
    page_table,
    suffix_lengths,
    suffix_prefix,
    decode_ages,
):
    head_dim = HEAD_SIZE
    page_len = PAGE_TOKENS
    q_scale = (D // QUERY_HEADS) ** (-0.5)
    tok_rows = suffix_query.shape[0]
    q_heads = suffix_query.shape[1] // head_dim
    kv_heads = suffix_key_value.shape[2] // head_dim
    query_group_width = q_heads // kv_heads
    blk_size = lax.axis_size("blk")
    my_index = lax.axis_index("blk")

    local_pages = prefix_page_store.shape[1]
    dq_rows = decode_query_rows.shape[0]
    kv_width = kv_heads * head_dim
    dq_lines = decode_query_rows.size // kv_width
    dkv_lines = decode_key_value.size // kv_width
    dec_local = jnp.concatenate(
        [
            decode_query_rows.reshape(dq_lines, kv_width),
            decode_key_value.reshape(dkv_lines, kv_width),
        ],
        axis=0,
    )
    dec_all = lax.all_to_all(
        jnp.broadcast_to(dec_local[None], (blk_size,) + dec_local.shape), "blk", 0, 0, tiled=False
    )
    all_dq = dec_all[:, :dq_lines].reshape(blk_size * dq_rows, q_heads * head_dim)
    all_dkv = (
        dec_all[:, dq_lines:]
        .reshape(blk_size, 2, dq_rows, kv_width)
        .transpose(1, 0, 2, 3)
        .reshape(2, blk_size * dq_rows, kv_width)
    )

    held_rows = local_pages * page_len
    piece = prefix_page_store.reshape(2, held_rows, kv_heads, head_dim).transpose(0, 2, 1, 3)
    gathered = lax.all_gather(piece, "blk", axis=0, tiled=False)

    look_back = 4
    pieces_back = [from_behind(suffix_key_value, "blk", d) for d in range(look_back, 0, -1)]
    window = jnp.concatenate(pieces_back + [suffix_key_value], axis=1)

    own_queries = suffix_query.reshape(tok_rows, kv_heads, query_group_width, head_dim)
    token_ids = my_index * tok_rows + jnp.arange(tok_rows, dtype=jnp.int32)
    tok_start, tok_prefix = token_tables(suffix_lengths, suffix_prefix, token_ids)
    key_ids = (my_index - look_back) * tok_rows + jnp.arange(
        (look_back + 1) * tok_rows, dtype=jnp.int32
    )
    visible = (key_ids[None, :] >= tok_start[:, None]) & (key_ids[None, :] <= token_ids[:, None])
    window_keys = window[0].reshape((look_back + 1) * tok_rows, kv_heads, head_dim)
    window_values = window[1].reshape((look_back + 1) * tok_rows, kv_heads, head_dim)
    own_numer, own_denom = attend(
        own_queries, window_keys, window_values, visible[:, None, None, :], q_scale
    )

    pool_pages = prefix_table.shape[0]
    per_prefix = PREFIX_LENGTH // PAGE_TOKENS
    page_owner = inverse_rows(prefix_table, jnp.arange(pool_pages, dtype=jnp.int32)) // per_prefix
    key_owner = jnp.repeat(page_owner, page_len)
    row_prefix = jnp.repeat(tok_prefix, query_group_width)
    rows_q = tok_rows * query_group_width
    chunks = 3
    chunk_keys = blk_size * held_rows // chunks
    sums = []
    for head in range(kv_heads):
        head_queries = own_queries[:, head].reshape(rows_q, head_dim)
        head_keys = gathered[:, 0, head].reshape(blk_size * held_rows, head_dim)
        head_values = gathered[:, 1, head].reshape(blk_size * held_rows, head_dim)
        numer_h = jnp.zeros((rows_q, head_dim), jnp.float32)
        denom_h = jnp.zeros((rows_q,), jnp.float32)
        for chunk in range(chunks):
            span = slice(chunk * chunk_keys, (chunk + 1) * chunk_keys)
            seen = row_prefix[:, None] == key_owner[span][None, :]
            numer_c, denom_c = attend_rows(
                head_queries, head_keys[span], head_values[span], seen, q_scale
            )
            numer_h = numer_h + numer_c
            denom_h = denom_h + denom_c
        sums.append((numer_h, denom_h))
    head_numer = [numer.reshape(tok_rows, query_group_width, head_dim) for numer, _ in sums]
    head_denom = [denom.reshape(tok_rows, query_group_width) for _, denom in sums]
    pre_numer = jnp.stack(head_numer, axis=1)
    pre_denom = jnp.stack(head_denom, axis=1)
    suffix_attn = ((own_numer + pre_numer) / (own_denom + pre_denom)[..., None]).astype(
        jnp.bfloat16
    )
    suffix_attn = suffix_attn.reshape(tok_rows, q_heads * head_dim)

    slot_total = all_dq.shape[0]
    slot_pages = SLOT_CAPACITY // PAGE_TOKENS
    local_cache = decode_page_store.shape[1]
    page_ids = my_index * local_cache + jnp.arange(local_cache, dtype=jnp.int32)
    position = inverse_rows(page_table, page_ids)
    slot_of = position // slot_pages
    block_of = position % slot_pages
    slot_hot = slot_of[:, None] == jnp.arange(slot_total, dtype=jnp.int32)[None, :]
    page_age = jnp.sum(slot_hot.astype(jnp.int32) * decode_ages[None, :], axis=1)
    select = slot_hot.astype(jnp.bfloat16)
    new_rows = jnp.einsum(
        "ls,tsc->tlc", select, all_dkv, preferred_element_type=jnp.float32
    ).astype(jnp.bfloat16)
    write_here = (block_of == page_age // page_len)[:, None] & (
        jnp.arange(page_len, dtype=jnp.int32)[None, :] == (page_age % page_len)[:, None]
    )
    new_cache = jnp.where(write_here[None, :, :, None], new_rows[:, :, None, :], decode_page_store)
    page_queries = jnp.dot(select, all_dq, preferred_element_type=jnp.float32).astype(jnp.bfloat16)
    page_queries = page_queries.reshape(local_cache, kv_heads, query_group_width, head_dim)
    key_cache = new_cache[0].reshape(local_cache, page_len, kv_heads, head_dim)
    value_cache = new_cache[1].reshape(local_cache, page_len, kv_heads, head_dim)
    logits = (
        jnp.einsum("lhgd,lphd->lhgp", page_queries, key_cache, preferred_element_type=jnp.float32)
        * q_scale
    )
    capped = soft_cap * jnp.tanh(logits / soft_cap)
    places = block_of[:, None] * page_len + jnp.arange(page_len, dtype=jnp.int32)[None, :]
    seen_pos = places <= page_age[:, None]
    weights = jnp.where(seen_pos[:, None, None, :], jnp.exp(capped), 0.0)
    page_denom = jnp.sum(weights, axis=3)
    page_numer = jnp.einsum(
        "lhgp,lphd->lhgd",
        weights.astype(jnp.bfloat16),
        value_cache,
        preferred_element_type=jnp.float32,
    )
    slot_float = slot_hot.astype(jnp.float32)
    page_sums = jnp.concatenate([page_numer, page_denom[..., None]], axis=3)
    slot_sums = jnp.einsum("ls,lhgd->shgd", slot_float, page_sums, precision=lax.Precision.HIGHEST)
    slot_sums = slot_sums.reshape((blk_size, slot_total // blk_size) + slot_sums.shape[1:])
    mine_sums = jnp.sum(lax.all_to_all(slot_sums, "blk", 0, 0, tiled=False), axis=0)
    mine_numer = mine_sums[..., :head_dim]
    mine_denom = mine_sums[..., head_dim]
    decode_attn = (mine_numer / mine_denom[..., None]).astype(jnp.bfloat16)
    decode_rows = decode_attn.shape[0]
    decode_attn = decode_attn.reshape(decode_rows, q_heads * head_dim)

    attention = jnp.concatenate([suffix_attn, decode_attn], axis=0)
    kv_size = lax.axis_size("kv")
    projected_t = jnp.einsum(
        "ko,rk->or", out_weight, attention, preferred_element_type=jnp.float32
    )
    residual = jnp.concatenate([suffix_resid, decode_resid], axis=0).astype(jnp.float32)
    shares = projected_t.astype(jnp.bfloat16).reshape(kv_size, -1, projected_t.shape[1])
    mine = jnp.sum(
        lax.all_to_all(shares, "kv", 0, 0, tiled=False).astype(jnp.float32), axis=0
    ).T
    squares = jnp.sum(mine * mine, axis=1)
    square_parts = lax.all_to_all(
        jnp.broadcast_to(squares[None], (kv_size,) + squares.shape), "kv", 0, 0, tiled=False
    )
    mean_square = jnp.sum(square_parts, axis=0) / D
    normed = mine * lax.rsqrt(mean_square + norm_eps)[:, None] * post_gain[None, :]
    hidden = (residual + normed).astype(jnp.bfloat16)
    return (hidden[:tok_rows], hidden[tok_rows:], new_cache)


def solution(mesh):
    placed = (
        P("blk", "kv"),
        P(None, "blk", "kv"),
        P("blk", "kv"),
        P("blk", "kv"),
        P(None, "blk", "kv"),
        P("blk", "kv"),
        P("kv", None),
        P("kv"),
        P(None, "blk", None, "kv"),
        P(),
        P(None, "blk", None, "kv"),
        P(),
        P(),
        P(),
        P(),
    )
    return jax.shard_map(
        body,
        mesh=mesh,
        in_specs=placed,
        out_specs=(P("blk", "kv"), P("blk", "kv"), P(None, "blk", None, "kv")),
        check_vma=False,
    )
```

```python
import functools
import math

import jax
import jax.numpy as jnp
from jax import lax
from jax.experimental import pallas as pl
from jax.experimental.pallas import tpu as pltpu
from jax.sharding import PartitionSpec as P

D = 4608
QUERY_HEADS = 32
HEAD_SIZE = 128
PAGE_TOKENS = 128
PREFIX_LENGTH = 3072
SLOT_CAPACITY = 1024


soft_cap = 50.0
norm_eps = 1e-06


def prefix_kernel(q_ref, k_ref, v_ref, own_ref, row_ref, num_ref, den_ref, *, q_scale, group):
    step = pl.program_id(1)

    @pl.when(step == 0)
    def _():
        num_ref[...] = jnp.zeros_like(num_ref)
        den_ref[...] = jnp.zeros_like(den_ref)

    q = q_ref[0]
    rows = row_ref[...]
    numer = num_ref[0]
    denom = den_ref[0]
    for part in range(group):
        k = k_ref[part, 0, 0]
        v = v_ref[part, 0, 0]
        s = lax.dot_general(q, k, (((1,), (1,)), ((), ())), preferred_element_type=jnp.float32)
        capped = soft_cap * jnp.tanh((s * q_scale) / soft_cap)
        seen = rows == own_ref[part]
        w = jnp.where(seen, jnp.exp(capped), 0.0)
        denom = denom + jnp.sum(w, axis=1, keepdims=True)
        numer = numer + jnp.dot(w.astype(jnp.bfloat16), v, preferred_element_type=jnp.float32)
    num_ref[0] = numer
    den_ref[0] = denom


def prefix_attention(q_heads, gathered, key_owner, row_prefix, q_scale, group=4, interpret=False):
    heads, rows_q, head_dim = q_heads.shape
    sources, _, _, held_rows, _ = gathered.shape
    steps = sources // group
    kern = functools.partial(prefix_kernel, q_scale=q_scale, group=group)
    return pl.pallas_call(
        kern,
        grid=(heads, steps),
        in_specs=[
            pl.BlockSpec((1, rows_q, head_dim), lambda h, j: (h, 0, 0)),
            pl.BlockSpec((group, 1, 1, held_rows, head_dim), lambda h, j: (j, 0, h, 0, 0)),
            pl.BlockSpec((group, 1, 1, held_rows, head_dim), lambda h, j: (j, 1, h, 0, 0)),
            pl.BlockSpec((group, 1, held_rows), lambda h, j: (j, 0, 0)),
            pl.BlockSpec((rows_q, 1), lambda h, j: (0, 0)),
        ],
        out_specs=[
            pl.BlockSpec((1, rows_q, head_dim), lambda h, j: (h, 0, 0)),
            pl.BlockSpec((1, rows_q, 1), lambda h, j: (h, 0, 0)),
        ],
        out_shape=[
            jax.ShapeDtypeStruct((heads, rows_q, head_dim), jnp.float32),
            jax.ShapeDtypeStruct((heads, rows_q, 1), jnp.float32),
        ],
        compiler_params=pltpu.CompilerParams(dimension_semantics=("parallel", "arbitrary")),
        interpret=interpret,
    )(q_heads, gathered, gathered, key_owner, row_prefix)


def from_behind(block, axis, distance):
    devices = range(lax.axis_size(axis))
    route = [(i - distance, i) for i in devices if i - distance in devices]
    return lax.ppermute(block, axis, route)


def attend(query_rows, key_rows, value_rows, visible, q_scale):
    logits = (
        jnp.einsum("qhgd,khd->qhgk", query_rows, key_rows, preferred_element_type=jnp.float32)
        * q_scale
    )
    capped = soft_cap * jnp.tanh(logits / soft_cap)
    weights = jnp.where(visible, jnp.exp(capped), 0.0)
    denominator = jnp.sum(weights, axis=3)
    numerator = jnp.einsum(
        "qhgk,khd->qhgd",
        weights.astype(jnp.bfloat16),
        value_rows,
        preferred_element_type=jnp.float32,
    )
    return (numerator, denominator)


def attend_rows(query_rows, key_rows, value_rows, visible, q_scale):
    logits = (
        jnp.dot(query_rows, key_rows.T, preferred_element_type=jnp.float32) * q_scale
    )
    capped = soft_cap * jnp.tanh(logits / soft_cap)
    weights = jnp.where(visible, jnp.exp(capped), 0.0)
    denominator = jnp.sum(weights, axis=1)
    numerator = jnp.dot(
        weights.astype(jnp.bfloat16), value_rows, preferred_element_type=jnp.float32
    )
    return (numerator, denominator)


def token_tables(lengths, prefix_ids, token_ids):
    suffix_ends = jnp.cumsum(lengths)
    starts = suffix_ends - lengths
    inside = (
        (token_ids[:, None] >= starts[None, :]) & (token_ids[:, None] < suffix_ends[None, :])
    ).astype(jnp.int32)
    tok_start = jnp.sum(inside * starts[None, :], axis=1)
    tok_prefix = jnp.sum(inside * prefix_ids[None, :], axis=1)
    return (tok_start, tok_prefix)


def inverse_rows(table, wanted):
    hits = (table[None, :] == wanted[:, None]).astype(jnp.int32)
    places = jnp.arange(table.shape[0], dtype=jnp.int32)
    return jnp.sum(hits * places[None, :], axis=1)


def body(
    suffix_query,
    suffix_key_value,
    suffix_resid,
    decode_query_rows,
    decode_key_value,
    decode_resid,
    out_weight,
    post_gain,
    prefix_page_store,
    prefix_table,
    decode_page_store,
    page_table,
    suffix_lengths,
    suffix_prefix,
    decode_ages,
):
    head_dim = HEAD_SIZE
    page_len = PAGE_TOKENS
    q_scale = (D // QUERY_HEADS) ** (-0.5)
    tok_rows = suffix_query.shape[0]
    q_heads = suffix_query.shape[1] // head_dim
    kv_heads = suffix_key_value.shape[2] // head_dim
    query_group_width = q_heads // kv_heads
    blk_size = lax.axis_size("blk")
    my_index = lax.axis_index("blk")

    local_pages = prefix_page_store.shape[1]
    dq_rows = decode_query_rows.shape[0]
    kv_width = kv_heads * head_dim
    dq_lines = decode_query_rows.size // kv_width
    dkv_lines = decode_key_value.size // kv_width
    dec_local = jnp.concatenate(
        [
            decode_query_rows.reshape(dq_lines, kv_width),
            decode_key_value.reshape(dkv_lines, kv_width),
        ],
        axis=0,
    )
    dec_all = lax.all_to_all(
        jnp.broadcast_to(dec_local[None], (blk_size,) + dec_local.shape), "blk", 0, 0, tiled=False
    )
    all_dq = dec_all[:, :dq_lines].reshape(blk_size * dq_rows, q_heads * head_dim)
    all_dkv = (
        dec_all[:, dq_lines:]
        .reshape(blk_size, 2, dq_rows, kv_width)
        .transpose(1, 0, 2, 3)
        .reshape(2, blk_size * dq_rows, kv_width)
    )

    held_rows = local_pages * page_len
    piece = prefix_page_store.reshape(2, held_rows, kv_heads, head_dim).transpose(0, 2, 1, 3)
    gathered = lax.all_gather(piece, "blk", axis=0, tiled=False)

    look_back = 4
    pieces_back = [from_behind(suffix_key_value, "blk", d) for d in range(look_back, 0, -1)]
    window = jnp.concatenate(pieces_back + [suffix_key_value], axis=1)

    own_queries = suffix_query.reshape(tok_rows, kv_heads, query_group_width, head_dim)
    token_ids = my_index * tok_rows + jnp.arange(tok_rows, dtype=jnp.int32)
    tok_start, tok_prefix = token_tables(suffix_lengths, suffix_prefix, token_ids)
    key_ids = (my_index - look_back) * tok_rows + jnp.arange(
        (look_back + 1) * tok_rows, dtype=jnp.int32
    )
    visible = (key_ids[None, :] >= tok_start[:, None]) & (key_ids[None, :] <= token_ids[:, None])
    window_keys = window[0].reshape((look_back + 1) * tok_rows, kv_heads, head_dim)
    window_values = window[1].reshape((look_back + 1) * tok_rows, kv_heads, head_dim)
    own_numer, own_denom = attend(
        own_queries, window_keys, window_values, visible[:, None, None, :], q_scale
    )

    pool_pages = prefix_table.shape[0]
    per_prefix = PREFIX_LENGTH // PAGE_TOKENS
    page_owner = inverse_rows(prefix_table, jnp.arange(pool_pages, dtype=jnp.int32)) // per_prefix
    key_owner = jnp.repeat(page_owner, page_len).reshape(blk_size, 1, held_rows)
    row_prefix = jnp.repeat(tok_prefix, query_group_width)[:, None]
    rows_q = tok_rows * query_group_width
    q_by_head = own_queries.transpose(1, 0, 2, 3).reshape(kv_heads, rows_q, head_dim)
    numer_p, denom_p = prefix_attention(q_by_head, gathered, key_owner, row_prefix, q_scale)
    pre_numer = numer_p.reshape(kv_heads, tok_rows, query_group_width, head_dim).transpose(
        1, 0, 2, 3
    )
    pre_denom = denom_p.reshape(kv_heads, tok_rows, query_group_width).transpose(1, 0, 2)
    suffix_attn = ((own_numer + pre_numer) / (own_denom + pre_denom)[..., None]).astype(
        jnp.bfloat16
    )
    suffix_attn = suffix_attn.reshape(tok_rows, q_heads * head_dim)

    slot_total = all_dq.shape[0]
    slot_pages = SLOT_CAPACITY // PAGE_TOKENS
    local_cache = decode_page_store.shape[1]
    page_ids = my_index * local_cache + jnp.arange(local_cache, dtype=jnp.int32)
    position = inverse_rows(page_table, page_ids)
    slot_of = position // slot_pages
    block_of = position % slot_pages
    slot_hot = slot_of[:, None] == jnp.arange(slot_total, dtype=jnp.int32)[None, :]
    page_age = jnp.sum(slot_hot.astype(jnp.int32) * decode_ages[None, :], axis=1)
    select = slot_hot.astype(jnp.bfloat16)
    new_rows = jnp.einsum(
        "ls,tsc->tlc", select, all_dkv, preferred_element_type=jnp.float32
    ).astype(jnp.bfloat16)
    write_here = (block_of == page_age // page_len)[:, None] & (
        jnp.arange(page_len, dtype=jnp.int32)[None, :] == (page_age % page_len)[:, None]
    )
    new_cache = jnp.where(write_here[None, :, :, None], new_rows[:, :, None, :], decode_page_store)
    page_queries = jnp.dot(select, all_dq, preferred_element_type=jnp.float32).astype(jnp.bfloat16)
    page_queries = page_queries.reshape(local_cache, kv_heads, query_group_width, head_dim)
    key_cache = new_cache[0].reshape(local_cache, page_len, kv_heads, head_dim)
    value_cache = new_cache[1].reshape(local_cache, page_len, kv_heads, head_dim)
    logits = (
        jnp.einsum("lhgd,lphd->lhgp", page_queries, key_cache, preferred_element_type=jnp.float32)
        * q_scale
    )
    capped = soft_cap * jnp.tanh(logits / soft_cap)
    places = block_of[:, None] * page_len + jnp.arange(page_len, dtype=jnp.int32)[None, :]
    seen_pos = places <= page_age[:, None]
    weights = jnp.where(seen_pos[:, None, None, :], jnp.exp(capped), 0.0)
    page_denom = jnp.sum(weights, axis=3)
    page_numer = jnp.einsum(
        "lhgp,lphd->lhgd",
        weights.astype(jnp.bfloat16),
        value_cache,
        preferred_element_type=jnp.float32,
    )
    slot_float = slot_hot.astype(jnp.float32)
    page_sums = jnp.concatenate([page_numer, page_denom[..., None]], axis=3)
    slot_sums = jnp.einsum("ls,lhgd->shgd", slot_float, page_sums, precision=lax.Precision.HIGHEST)
    slot_sums = slot_sums.reshape((blk_size, slot_total // blk_size) + slot_sums.shape[1:])
    mine_sums = jnp.sum(lax.all_to_all(slot_sums, "blk", 0, 0, tiled=False), axis=0)
    mine_numer = mine_sums[..., :head_dim]
    mine_denom = mine_sums[..., head_dim]
    decode_attn = (mine_numer / mine_denom[..., None]).astype(jnp.bfloat16)
    decode_rows = decode_attn.shape[0]
    decode_attn = decode_attn.reshape(decode_rows, q_heads * head_dim)

    attention = jnp.concatenate([suffix_attn, decode_attn], axis=0)
    kv_size = lax.axis_size("kv")
    projected_t = jnp.einsum(
        "ko,rk->or", out_weight, attention, preferred_element_type=jnp.float32
    )
    residual = jnp.concatenate([suffix_resid, decode_resid], axis=0).astype(jnp.float32)
    shares = projected_t.astype(jnp.bfloat16).reshape(kv_size, -1, projected_t.shape[1])
    mine = jnp.sum(
        lax.all_to_all(shares, "kv", 0, 0, tiled=False).astype(jnp.float32), axis=0
    ).T
    squares = jnp.sum(mine * mine, axis=1)
    square_parts = lax.all_to_all(
        jnp.broadcast_to(squares[None], (kv_size,) + squares.shape), "kv", 0, 0, tiled=False
    )
    mean_square = jnp.sum(square_parts, axis=0) / D
    normed = mine * lax.rsqrt(mean_square + norm_eps)[:, None] * post_gain[None, :]
    hidden = (residual + normed).astype(jnp.bfloat16)
    return (hidden[:tok_rows], hidden[tok_rows:], new_cache)


def solution(mesh):
    placed = (
        P("blk", "kv"),
        P(None, "blk", "kv"),
        P("blk", "kv"),
        P("blk", "kv"),
        P(None, "blk", "kv"),
        P("blk", "kv"),
        P("kv", None),
        P("kv"),
        P(None, "blk", None, "kv"),
        P(),
        P(None, "blk", None, "kv"),
        P(),
        P(),
        P(),
        P(),
    )
    return jax.shard_map(
        body,
        mesh=mesh,
        in_specs=placed,
        out_specs=(P("blk", "kv"), P("blk", "kv"), P(None, "blk", None, "kv")),
        check_vma=False,
    )
```

```python
import functools
import math

import jax
import jax.numpy as jnp
from jax import lax
from jax.experimental import pallas as pl
from jax.experimental.pallas import tpu as pltpu
from jax.sharding import PartitionSpec as P

D = 4608
QUERY_HEADS = 32
HEAD_SIZE = 128
PAGE_TOKENS = 128
PREFIX_LENGTH = 3072
SLOT_CAPACITY = 1024


soft_cap = 50.0
norm_eps = 1e-06


def prefix_kernel(q_ref, k_ref, v_ref, own_ref, row_ref, num_ref, den_ref, *, q_scale, group):
    step = pl.program_id(1)

    @pl.when(step == 0)
    def _():
        num_ref[...] = jnp.zeros_like(num_ref)
        den_ref[...] = jnp.zeros_like(den_ref)

    q = q_ref[0]
    rows = row_ref[...]
    numer = num_ref[0]
    denom = den_ref[0]
    for part in range(group):
        k = k_ref[part, 0, 0]
        v = v_ref[part, 0, 0]
        s = lax.dot_general(q, k, (((1,), (1,)), ((), ())), preferred_element_type=jnp.float32)
        capped = soft_cap * jnp.tanh(s * (q_scale / soft_cap))
        seen = rows == own_ref[part]
        w = jnp.where(seen, jnp.exp(capped), 0.0)
        denom = denom + jnp.sum(w, axis=1, keepdims=True)
        numer = numer + jnp.dot(w.astype(jnp.bfloat16), v, preferred_element_type=jnp.float32)
    num_ref[0] = numer
    den_ref[0] = denom


def prefix_attention(q_heads, gathered, key_owner, row_prefix, q_scale, group=8):
    heads, rows_q, head_dim = q_heads.shape
    sources, _, _, held_rows, _ = gathered.shape
    steps = sources // group
    kern = functools.partial(prefix_kernel, q_scale=q_scale, group=group)
    return pl.pallas_call(
        kern,
        grid=(heads, steps),
        in_specs=[
            pl.BlockSpec((1, rows_q, head_dim), lambda h, j: (h, 0, 0)),
            pl.BlockSpec((group, 1, 1, held_rows, head_dim), lambda h, j: (j, 0, h, 0, 0)),
            pl.BlockSpec((group, 1, 1, held_rows, head_dim), lambda h, j: (j, 1, h, 0, 0)),
            pl.BlockSpec((group, 1, held_rows), lambda h, j: (j, 0, 0)),
            pl.BlockSpec((rows_q, 1), lambda h, j: (0, 0)),
        ],
        out_specs=[
            pl.BlockSpec((1, rows_q, head_dim), lambda h, j: (h, 0, 0)),
            pl.BlockSpec((1, rows_q, 1), lambda h, j: (h, 0, 0)),
        ],
        out_shape=[
            jax.ShapeDtypeStruct((heads, rows_q, head_dim), jnp.float32),
            jax.ShapeDtypeStruct((heads, rows_q, 1), jnp.float32),
        ],
        compiler_params=pltpu.CompilerParams(dimension_semantics=("parallel", "arbitrary")),
    )(q_heads, gathered, gathered, key_owner, row_prefix)


def from_behind(block, axis, distance):
    devices = range(lax.axis_size(axis))
    route = [(i - distance, i) for i in devices if i - distance in devices]
    return lax.ppermute(block, axis, route)


def attend(query_rows, key_rows, value_rows, visible, q_scale):
    logits = (
        jnp.einsum("qhgd,khd->qhgk", query_rows, key_rows, preferred_element_type=jnp.float32)
        * q_scale
    )
    capped = soft_cap * jnp.tanh(logits / soft_cap)
    weights = jnp.where(visible, jnp.exp(capped), 0.0)
    denominator = jnp.sum(weights, axis=3)
    numerator = jnp.einsum(
        "qhgk,khd->qhgd",
        weights.astype(jnp.bfloat16),
        value_rows,
        preferred_element_type=jnp.float32,
    )
    return (numerator, denominator)


def token_tables(lengths, prefix_ids, token_ids):
    suffix_ends = jnp.cumsum(lengths)
    starts = suffix_ends - lengths
    inside = (
        (token_ids[:, None] >= starts[None, :]) & (token_ids[:, None] < suffix_ends[None, :])
    ).astype(jnp.int32)
    tok_start = jnp.sum(inside * starts[None, :], axis=1)
    tok_prefix = jnp.sum(inside * prefix_ids[None, :], axis=1)
    return (tok_start, tok_prefix)


def inverse_rows(table, wanted):
    hits = (table[None, :] == wanted[:, None]).astype(jnp.int32)
    places = jnp.arange(table.shape[0], dtype=jnp.int32)
    return jnp.sum(hits * places[None, :], axis=1)


def body(
    suffix_query,
    suffix_key_value,
    suffix_resid,
    decode_query_rows,
    decode_key_value,
    decode_resid,
    out_weight,
    post_gain,
    prefix_page_store,
    prefix_table,
    decode_page_store,
    page_table,
    suffix_lengths,
    suffix_prefix,
    decode_ages,
):
    head_dim = HEAD_SIZE
    page_len = PAGE_TOKENS
    q_scale = (D // QUERY_HEADS) ** (-0.5)
    tok_rows = suffix_query.shape[0]
    q_heads = suffix_query.shape[1] // head_dim
    kv_heads = suffix_key_value.shape[2] // head_dim
    query_group_width = q_heads // kv_heads
    blk_size = lax.axis_size("blk")
    my_index = lax.axis_index("blk")

    local_pages = prefix_page_store.shape[1]
    dq_rows = decode_query_rows.shape[0]
    kv_width = kv_heads * head_dim
    dq_lines = decode_query_rows.size // kv_width
    dkv_lines = decode_key_value.size // kv_width
    dec_local = jnp.concatenate(
        [
            decode_query_rows.reshape(dq_lines, kv_width),
            decode_key_value.reshape(dkv_lines, kv_width),
        ],
        axis=0,
    )
    dec_all = lax.all_to_all(
        jnp.broadcast_to(dec_local[None], (blk_size,) + dec_local.shape), "blk", 0, 0, tiled=False
    )
    all_dq = dec_all[:, :dq_lines].reshape(blk_size * dq_rows, q_heads * head_dim)
    all_dkv = (
        dec_all[:, dq_lines:]
        .reshape(blk_size, 2, dq_rows, kv_width)
        .transpose(1, 0, 2, 3)
        .reshape(2, blk_size * dq_rows, kv_width)
    )

    held_rows = local_pages * page_len
    piece = prefix_page_store.reshape(2, held_rows, kv_heads, head_dim).transpose(0, 2, 1, 3)
    gathered = lax.all_gather(piece, "blk", axis=0, tiled=False)

    look_back = 4
    pieces_back = [from_behind(suffix_key_value, "blk", d) for d in range(look_back, 0, -1)]
    window = jnp.concatenate(pieces_back + [suffix_key_value], axis=1)

    own_queries = suffix_query.reshape(tok_rows, kv_heads, query_group_width, head_dim)
    token_ids = my_index * tok_rows + jnp.arange(tok_rows, dtype=jnp.int32)
    tok_start, tok_prefix = token_tables(suffix_lengths, suffix_prefix, token_ids)
    key_ids = (my_index - look_back) * tok_rows + jnp.arange(
        (look_back + 1) * tok_rows, dtype=jnp.int32
    )
    visible = (key_ids[None, :] >= tok_start[:, None]) & (key_ids[None, :] <= token_ids[:, None])
    window_keys = window[0].reshape((look_back + 1) * tok_rows, kv_heads, head_dim)
    window_values = window[1].reshape((look_back + 1) * tok_rows, kv_heads, head_dim)
    own_numer, own_denom = attend(
        own_queries, window_keys, window_values, visible[:, None, None, :], q_scale
    )

    pool_pages = prefix_table.shape[0]
    per_prefix = PREFIX_LENGTH // PAGE_TOKENS
    page_owner = inverse_rows(prefix_table, jnp.arange(pool_pages, dtype=jnp.int32)) // per_prefix
    key_owner = jnp.repeat(page_owner, page_len).reshape(blk_size, 1, held_rows)
    row_prefix = jnp.repeat(tok_prefix, query_group_width)[:, None]
    rows_q = tok_rows * query_group_width
    q_by_head = own_queries.transpose(1, 0, 2, 3).reshape(kv_heads, rows_q, head_dim)
    numer_p, denom_p = prefix_attention(q_by_head, gathered, key_owner, row_prefix, q_scale)
    pre_numer = numer_p.reshape(kv_heads, tok_rows, query_group_width, head_dim).transpose(
        1, 0, 2, 3
    )
    pre_denom = denom_p.reshape(kv_heads, tok_rows, query_group_width).transpose(1, 0, 2)
    suffix_attn = ((own_numer + pre_numer) / (own_denom + pre_denom)[..., None]).astype(
        jnp.bfloat16
    )
    suffix_attn = suffix_attn.reshape(tok_rows, q_heads * head_dim)

    slot_total = all_dq.shape[0]
    slot_pages = SLOT_CAPACITY // PAGE_TOKENS
    local_cache = decode_page_store.shape[1]
    page_ids = my_index * local_cache + jnp.arange(local_cache, dtype=jnp.int32)
    position = inverse_rows(page_table, page_ids)
    slot_of = position // slot_pages
    block_of = position % slot_pages
    slot_hot = slot_of[:, None] == jnp.arange(slot_total, dtype=jnp.int32)[None, :]
    page_age = jnp.sum(slot_hot.astype(jnp.int32) * decode_ages[None, :], axis=1)
    select = slot_hot.astype(jnp.bfloat16)
    new_rows = jnp.einsum(
        "ls,tsc->tlc", select, all_dkv, preferred_element_type=jnp.float32
    ).astype(jnp.bfloat16)
    write_here = (block_of == page_age // page_len)[:, None] & (
        jnp.arange(page_len, dtype=jnp.int32)[None, :] == (page_age % page_len)[:, None]
    )
    new_cache = jnp.where(write_here[None, :, :, None], new_rows[:, :, None, :], decode_page_store)
    page_queries = jnp.dot(select, all_dq, preferred_element_type=jnp.float32).astype(jnp.bfloat16)
    page_queries = page_queries.reshape(local_cache, kv_heads, query_group_width, head_dim)
    key_cache = new_cache[0].reshape(local_cache, page_len, kv_heads, head_dim)
    value_cache = new_cache[1].reshape(local_cache, page_len, kv_heads, head_dim)
    logits = (
        jnp.einsum("lhgd,lphd->lhgp", page_queries, key_cache, preferred_element_type=jnp.float32)
        * q_scale
    )
    capped = soft_cap * jnp.tanh(logits / soft_cap)
    places = block_of[:, None] * page_len + jnp.arange(page_len, dtype=jnp.int32)[None, :]
    seen_pos = places <= page_age[:, None]
    weights = jnp.where(seen_pos[:, None, None, :], jnp.exp(capped), 0.0)
    page_denom = jnp.sum(weights, axis=3)
    page_numer = jnp.einsum(
        "lhgp,lphd->lhgd",
        weights.astype(jnp.bfloat16),
        value_cache,
        preferred_element_type=jnp.float32,
    )
    slot_float = slot_hot.astype(jnp.float32)
    page_sums = jnp.concatenate([page_numer, page_denom[..., None]], axis=3)
    slot_sums = jnp.einsum("ls,lhgd->shgd", slot_float, page_sums, precision=lax.Precision.HIGHEST)
    slot_sums = slot_sums.reshape((blk_size, slot_total // blk_size) + slot_sums.shape[1:])
    mine_sums = jnp.sum(lax.all_to_all(slot_sums, "blk", 0, 0, tiled=False), axis=0)
    mine_numer = mine_sums[..., :head_dim]
    mine_denom = mine_sums[..., head_dim]
    decode_attn = (mine_numer / mine_denom[..., None]).astype(jnp.bfloat16)
    decode_rows = decode_attn.shape[0]
    decode_attn = decode_attn.reshape(decode_rows, q_heads * head_dim)

    attention = jnp.concatenate([suffix_attn, decode_attn], axis=0)
    kv_size = lax.axis_size("kv")
    projected_t = jnp.einsum(
        "ko,rk->or", out_weight, attention, preferred_element_type=jnp.float32
    )
    residual = jnp.concatenate([suffix_resid, decode_resid], axis=0).astype(jnp.float32)
    shares = projected_t.astype(jnp.bfloat16).reshape(kv_size, -1, projected_t.shape[1])
    mine = jnp.sum(
        lax.all_to_all(shares, "kv", 0, 0, tiled=False).astype(jnp.float32), axis=0
    ).T
    squares = jnp.sum(mine * mine, axis=1)
    square_parts = lax.all_to_all(
        jnp.broadcast_to(squares[None], (kv_size,) + squares.shape), "kv", 0, 0, tiled=False
    )
    mean_square = jnp.sum(square_parts, axis=0) / D
    normed = mine * lax.rsqrt(mean_square + norm_eps)[:, None] * post_gain[None, :]
    hidden = (residual + normed).astype(jnp.bfloat16)
    return (hidden[:tok_rows], hidden[tok_rows:], new_cache)


def solution(mesh):
    placed = (
        P("blk", "kv"),
        P(None, "blk", "kv"),
        P("blk", "kv"),
        P("blk", "kv"),
        P(None, "blk", "kv"),
        P("blk", "kv"),
        P("kv", None),
        P("kv"),
        P(None, "blk", None, "kv"),
        P(),
        P(None, "blk", None, "kv"),
        P(),
        P(),
        P(),
        P(),
    )
    return jax.shard_map(
        body,
        mesh=mesh,
        in_specs=placed,
        out_specs=(P("blk", "kv"), P("blk", "kv"), P(None, "blk", None, "kv")),
        check_vma=False,
    )
```

```python
import functools
import math

import jax
import jax.numpy as jnp
from jax import lax
from jax.experimental import pallas as pl
from jax.experimental.pallas import tpu as pltpu
from jax.sharding import PartitionSpec as P

D = 4608
QUERY_HEADS = 32
HEAD_SIZE = 128
PAGE_TOKENS = 128
PREFIX_LENGTH = 3072
SLOT_CAPACITY = 1024


soft_cap = 50.0
norm_eps = 1e-06


def prefix_kernel(q_ref, k_ref, v_ref, own_ref, row_ref, num_ref, den_ref, *, q_scale, group):
    step = pl.program_id(1)

    @pl.when(step == 0)
    def _():
        num_ref[...] = jnp.zeros_like(num_ref)
        den_ref[...] = jnp.zeros_like(den_ref)

    q = q_ref[0]
    rows = row_ref[...]
    numer = num_ref[0]
    denom = den_ref[0]
    for part in range(group):
        k = k_ref[part, 0, 0]
        v = v_ref[part, 0, 0]
        s = lax.dot_general(q, k, (((1,), (1,)), ((), ())), preferred_element_type=jnp.float32)
        capped = soft_cap * jnp.tanh(s * (q_scale / soft_cap))
        seen = rows == own_ref[part]
        w = jnp.where(seen, jnp.exp(capped), 0.0)
        denom = denom + jnp.sum(w, axis=1, keepdims=True)
        numer = numer + jnp.dot(w.astype(jnp.bfloat16), v, preferred_element_type=jnp.float32)
    num_ref[0] = numer
    den_ref[0] = denom


def prefix_attention(q_heads, gathered, key_owner, row_prefix, q_scale, group=8):
    heads, rows_q, head_dim = q_heads.shape
    sources, _, _, held_rows, _ = gathered.shape
    steps = sources // group
    kern = functools.partial(prefix_kernel, q_scale=q_scale, group=group)
    return pl.pallas_call(
        kern,
        grid=(heads, steps),
        in_specs=[
            pl.BlockSpec((1, rows_q, head_dim), lambda h, j: (h, 0, 0)),
            pl.BlockSpec((group, 1, 1, held_rows, head_dim), lambda h, j: (j, 0, h, 0, 0)),
            pl.BlockSpec((group, 1, 1, held_rows, head_dim), lambda h, j: (j, 1, h, 0, 0)),
            pl.BlockSpec((group, 1, held_rows), lambda h, j: (j, 0, 0)),
            pl.BlockSpec((rows_q, 1), lambda h, j: (0, 0)),
        ],
        out_specs=[
            pl.BlockSpec((1, rows_q, head_dim), lambda h, j: (h, 0, 0)),
            pl.BlockSpec((1, rows_q, 1), lambda h, j: (h, 0, 0)),
        ],
        out_shape=[
            jax.ShapeDtypeStruct((heads, rows_q, head_dim), jnp.float32),
            jax.ShapeDtypeStruct((heads, rows_q, 1), jnp.float32),
        ],
        compiler_params=pltpu.CompilerParams(dimension_semantics=("parallel", "arbitrary")),
    )(q_heads, gathered, gathered, key_owner, row_prefix)


def from_behind(block, axis, distance):
    devices = range(lax.axis_size(axis))
    route = [(i - distance, i) for i in devices if i - distance in devices]
    return lax.ppermute(block, axis, route)


def attend(query_rows, key_rows, value_rows, visible, q_scale):
    logits = (
        jnp.einsum("qhgd,khd->qhgk", query_rows, key_rows, preferred_element_type=jnp.float32)
        * q_scale
    )
    capped = soft_cap * jnp.tanh(logits / soft_cap)
    weights = jnp.where(visible, jnp.exp(capped), 0.0)
    denominator = jnp.sum(weights, axis=3)
    numerator = jnp.einsum(
        "qhgk,khd->qhgd",
        weights.astype(jnp.bfloat16),
        value_rows,
        preferred_element_type=jnp.float32,
    )
    return (numerator, denominator)


def token_tables(lengths, prefix_ids, token_ids):
    suffix_ends = jnp.cumsum(lengths)
    starts = suffix_ends - lengths
    inside = (
        (token_ids[:, None] >= starts[None, :]) & (token_ids[:, None] < suffix_ends[None, :])
    ).astype(jnp.int32)
    tok_start = jnp.sum(inside * starts[None, :], axis=1)
    tok_prefix = jnp.sum(inside * prefix_ids[None, :], axis=1)
    return (tok_start, tok_prefix)


def inverse_rows(table, wanted):
    hits = (table[None, :] == wanted[:, None]).astype(jnp.int32)
    places = jnp.arange(table.shape[0], dtype=jnp.int32)
    return jnp.sum(hits * places[None, :], axis=1)


def body(
    suffix_query,
    suffix_key_value,
    suffix_resid,
    decode_query_rows,
    decode_key_value,
    decode_resid,
    out_weight,
    post_gain,
    prefix_page_store,
    prefix_table,
    decode_page_store,
    page_table,
    suffix_lengths,
    suffix_prefix,
    decode_ages,
):
    head_dim = HEAD_SIZE
    page_len = PAGE_TOKENS
    q_scale = (D // QUERY_HEADS) ** (-0.5)
    tok_rows = suffix_query.shape[0]
    q_heads = suffix_query.shape[1] // head_dim
    kv_heads = suffix_key_value.shape[2] // head_dim
    query_group_width = q_heads // kv_heads
    blk_size = lax.axis_size("blk")
    my_index = lax.axis_index("blk")

    local_pages = prefix_page_store.shape[1]
    dq_rows = decode_query_rows.shape[0]
    kv_width = kv_heads * head_dim
    dq_lines = decode_query_rows.size // kv_width
    dkv_lines = decode_key_value.size // kv_width
    dec_local = jnp.concatenate(
        [
            decode_query_rows.reshape(dq_lines, kv_width),
            decode_key_value.reshape(dkv_lines, kv_width),
        ],
        axis=0,
    )
    dec_all = lax.all_to_all(
        jnp.broadcast_to(dec_local[None], (blk_size,) + dec_local.shape), "blk", 0, 0, tiled=False
    )
    all_dq = dec_all[:, :dq_lines].reshape(blk_size * dq_rows, q_heads * head_dim)
    all_dkv = (
        dec_all[:, dq_lines:]
        .reshape(blk_size, 2, dq_rows, kv_width)
        .transpose(1, 0, 2, 3)
        .reshape(2, blk_size * dq_rows, kv_width)
    )

    held_rows = local_pages * page_len
    piece = prefix_page_store.reshape(2, held_rows, kv_heads, head_dim).transpose(0, 2, 1, 3)
    gathered = lax.all_gather(piece, "blk", axis=0, tiled=False)

    kv_size = lax.axis_size("kv")
    out_cols = out_weight.shape[1] // kv_size
    weight_blocks = out_weight.reshape(out_weight.shape[0], kv_size, out_cols).transpose(1, 0, 2)
    my_weight = lax.all_to_all(weight_blocks, "kv", 0, 0, tiled=False)

    look_back = 4
    pieces_back = [from_behind(suffix_key_value, "blk", d) for d in range(look_back, 0, -1)]
    window = jnp.concatenate(pieces_back + [suffix_key_value], axis=1)

    own_queries = suffix_query.reshape(tok_rows, kv_heads, query_group_width, head_dim)
    token_ids = my_index * tok_rows + jnp.arange(tok_rows, dtype=jnp.int32)
    tok_start, tok_prefix = token_tables(suffix_lengths, suffix_prefix, token_ids)
    key_ids = (my_index - look_back) * tok_rows + jnp.arange(
        (look_back + 1) * tok_rows, dtype=jnp.int32
    )
    visible = (key_ids[None, :] >= tok_start[:, None]) & (key_ids[None, :] <= token_ids[:, None])
    window_keys = window[0].reshape((look_back + 1) * tok_rows, kv_heads, head_dim)
    window_values = window[1].reshape((look_back + 1) * tok_rows, kv_heads, head_dim)
    own_numer, own_denom = attend(
        own_queries, window_keys, window_values, visible[:, None, None, :], q_scale
    )

    pool_pages = prefix_table.shape[0]
    per_prefix = PREFIX_LENGTH // PAGE_TOKENS
    page_owner = inverse_rows(prefix_table, jnp.arange(pool_pages, dtype=jnp.int32)) // per_prefix
    key_owner = jnp.repeat(page_owner, page_len).reshape(blk_size, 1, held_rows)
    row_prefix = jnp.repeat(tok_prefix, query_group_width)[:, None]
    rows_q = tok_rows * query_group_width
    q_by_head = own_queries.transpose(1, 0, 2, 3).reshape(kv_heads, rows_q, head_dim)
    numer_p, denom_p = prefix_attention(q_by_head, gathered, key_owner, row_prefix, q_scale)
    pre_numer = numer_p.reshape(kv_heads, tok_rows, query_group_width, head_dim).transpose(
        1, 0, 2, 3
    )
    pre_denom = denom_p.reshape(kv_heads, tok_rows, query_group_width).transpose(1, 0, 2)
    suffix_attn = ((own_numer + pre_numer) / (own_denom + pre_denom)[..., None]).astype(
        jnp.bfloat16
    )
    suffix_attn = suffix_attn.reshape(tok_rows, q_heads * head_dim)

    slot_total = all_dq.shape[0]
    slot_pages = SLOT_CAPACITY // PAGE_TOKENS
    local_cache = decode_page_store.shape[1]
    page_ids = my_index * local_cache + jnp.arange(local_cache, dtype=jnp.int32)
    position = inverse_rows(page_table, page_ids)
    slot_of = position // slot_pages
    block_of = position % slot_pages
    slot_hot = slot_of[:, None] == jnp.arange(slot_total, dtype=jnp.int32)[None, :]
    page_age = jnp.sum(slot_hot.astype(jnp.int32) * decode_ages[None, :], axis=1)
    select = slot_hot.astype(jnp.bfloat16)
    new_rows = jnp.einsum(
        "ls,tsc->tlc", select, all_dkv, preferred_element_type=jnp.float32
    ).astype(jnp.bfloat16)
    write_here = (block_of == page_age // page_len)[:, None] & (
        jnp.arange(page_len, dtype=jnp.int32)[None, :] == (page_age % page_len)[:, None]
    )
    new_cache = jnp.where(write_here[None, :, :, None], new_rows[:, :, None, :], decode_page_store)
    page_queries = jnp.dot(select, all_dq, preferred_element_type=jnp.float32).astype(jnp.bfloat16)
    page_queries = page_queries.reshape(local_cache, kv_heads, query_group_width, head_dim)
    key_cache = new_cache[0].reshape(local_cache, page_len, kv_heads, head_dim)
    value_cache = new_cache[1].reshape(local_cache, page_len, kv_heads, head_dim)
    logits = (
        jnp.einsum("lhgd,lphd->lhgp", page_queries, key_cache, preferred_element_type=jnp.float32)
        * q_scale
    )
    capped = soft_cap * jnp.tanh(logits / soft_cap)
    places = block_of[:, None] * page_len + jnp.arange(page_len, dtype=jnp.int32)[None, :]
    seen_pos = places <= page_age[:, None]
    weights = jnp.where(seen_pos[:, None, None, :], jnp.exp(capped), 0.0)
    page_denom = jnp.sum(weights, axis=3)
    page_numer = jnp.einsum(
        "lhgp,lphd->lhgd",
        weights.astype(jnp.bfloat16),
        value_cache,
        preferred_element_type=jnp.float32,
    )
    slot_float = slot_hot.astype(jnp.float32)
    page_sums = jnp.concatenate([page_numer, page_denom[..., None]], axis=3)
    slot_sums = jnp.einsum("ls,lhgd->shgd", slot_float, page_sums, precision=lax.Precision.HIGHEST)
    slot_sums = slot_sums.reshape((blk_size, slot_total // blk_size) + slot_sums.shape[1:])
    mine_sums = jnp.sum(lax.all_to_all(slot_sums, "blk", 0, 0, tiled=False), axis=0)
    mine_numer = mine_sums[..., :head_dim]
    mine_denom = mine_sums[..., head_dim]
    decode_attn = (mine_numer / mine_denom[..., None]).astype(jnp.bfloat16)
    decode_rows = decode_attn.shape[0]
    decode_attn = decode_attn.reshape(decode_rows, q_heads * head_dim)

    attention = jnp.concatenate([suffix_attn, decode_attn], axis=0)
    kv_size = lax.axis_size("kv")
    residual = jnp.concatenate([suffix_resid, decode_resid], axis=0).astype(jnp.float32)
    heard = lax.all_to_all(
        jnp.broadcast_to(attention[None], (kv_size,) + attention.shape), "kv", 0, 0, tiled=False
    )
    mine = jnp.einsum("srk,sko->ro", heard, my_weight, preferred_element_type=jnp.float32)
    squares = jnp.sum(mine * mine, axis=1)
    square_parts = lax.all_to_all(
        jnp.broadcast_to(squares[None], (kv_size,) + squares.shape), "kv", 0, 0, tiled=False
    )
    mean_square = jnp.sum(square_parts, axis=0) / D
    normed = mine * lax.rsqrt(mean_square + norm_eps)[:, None] * post_gain[None, :]
    hidden = (residual + normed).astype(jnp.bfloat16)
    return (hidden[:tok_rows], hidden[tok_rows:], new_cache)


def solution(mesh):
    placed = (
        P("blk", "kv"),
        P(None, "blk", "kv"),
        P("blk", "kv"),
        P("blk", "kv"),
        P(None, "blk", "kv"),
        P("blk", "kv"),
        P("kv", None),
        P("kv"),
        P(None, "blk", None, "kv"),
        P(),
        P(None, "blk", None, "kv"),
        P(),
        P(),
        P(),
        P(),
    )
    return jax.shard_map(
        body,
        mesh=mesh,
        in_specs=placed,
        out_specs=(P("blk", "kv"), P("blk", "kv"), P(None, "blk", None, "kv")),
        check_vma=False,
    )
```

```python
import functools
import math

import jax
import jax.numpy as jnp
from jax import lax
from jax.experimental import pallas as pl
from jax.experimental.pallas import tpu as pltpu
from jax.sharding import PartitionSpec as P

D = 4608
QUERY_HEADS = 32
HEAD_SIZE = 128
PAGE_TOKENS = 128
PREFIX_LENGTH = 3072
SLOT_CAPACITY = 1024


soft_cap = 50.0
norm_eps = 1e-06


def prefix_kernel(q_ref, k_ref, v_ref, own_ref, row_ref, num_ref, den_ref, *, q_scale, group):
    step = pl.program_id(1)

    @pl.when(step == 0)
    def _():
        num_ref[...] = jnp.zeros_like(num_ref)
        den_ref[...] = jnp.zeros_like(den_ref)

    q = q_ref[0]
    rows = row_ref[...]
    numer = num_ref[0]
    denom = den_ref[0]
    for part in range(group):
        k = k_ref[part, 0, 0]
        v = v_ref[part, 0, 0]
        s = lax.dot_general(q, k, (((1,), (1,)), ((), ())), preferred_element_type=jnp.float32)
        capped = soft_cap * jnp.tanh(s * (q_scale / soft_cap))
        seen = rows == own_ref[part]
        w = jnp.where(seen, jnp.exp(capped), 0.0)
        denom = denom + jnp.sum(w, axis=1, keepdims=True)
        numer = numer + jnp.dot(w.astype(jnp.bfloat16), v, preferred_element_type=jnp.float32)
    num_ref[0] = numer
    den_ref[0] = denom


def prefix_attention(q_heads, gathered, key_owner, row_prefix, q_scale, group=8):
    heads, rows_q, head_dim = q_heads.shape
    sources, _, _, held_rows, _ = gathered.shape
    steps = sources // group
    kern = functools.partial(prefix_kernel, q_scale=q_scale, group=group)
    return pl.pallas_call(
        kern,
        grid=(heads, steps),
        in_specs=[
            pl.BlockSpec((1, rows_q, head_dim), lambda h, j: (h, 0, 0)),
            pl.BlockSpec((group, 1, 1, held_rows, head_dim), lambda h, j: (j, 0, h, 0, 0)),
            pl.BlockSpec((group, 1, 1, held_rows, head_dim), lambda h, j: (j, 1, h, 0, 0)),
            pl.BlockSpec((group, 1, held_rows), lambda h, j: (j, 0, 0)),
            pl.BlockSpec((rows_q, 1), lambda h, j: (0, 0)),
        ],
        out_specs=[
            pl.BlockSpec((1, rows_q, head_dim), lambda h, j: (h, 0, 0)),
            pl.BlockSpec((1, rows_q, 1), lambda h, j: (h, 0, 0)),
        ],
        out_shape=[
            jax.ShapeDtypeStruct((heads, rows_q, head_dim), jnp.float32),
            jax.ShapeDtypeStruct((heads, rows_q, 1), jnp.float32),
        ],
        compiler_params=pltpu.CompilerParams(dimension_semantics=("parallel", "arbitrary")),
    )(q_heads, gathered, gathered, key_owner, row_prefix)


def from_behind(block, axis, distance):
    devices = range(lax.axis_size(axis))
    route = [(i - distance, i) for i in devices if i - distance in devices]
    return lax.ppermute(block, axis, route)


def attend(query_rows, key_rows, value_rows, visible, q_scale):
    logits = (
        jnp.einsum("qhgd,khd->qhgk", query_rows, key_rows, preferred_element_type=jnp.float32)
        * q_scale
    )
    capped = soft_cap * jnp.tanh(logits / soft_cap)
    weights = jnp.where(visible, jnp.exp(capped), 0.0)
    denominator = jnp.sum(weights, axis=3)
    numerator = jnp.einsum(
        "qhgk,khd->qhgd",
        weights.astype(jnp.bfloat16),
        value_rows,
        preferred_element_type=jnp.float32,
    )
    return (numerator, denominator)


def token_tables(lengths, prefix_ids, token_ids):
    suffix_ends = jnp.cumsum(lengths)
    starts = suffix_ends - lengths
    inside = (
        (token_ids[:, None] >= starts[None, :]) & (token_ids[:, None] < suffix_ends[None, :])
    ).astype(jnp.int32)
    tok_start = jnp.sum(inside * starts[None, :], axis=1)
    tok_prefix = jnp.sum(inside * prefix_ids[None, :], axis=1)
    return (tok_start, tok_prefix)


def inverse_rows(table, wanted):
    hits = (table[None, :] == wanted[:, None]).astype(jnp.int32)
    places = jnp.arange(table.shape[0], dtype=jnp.int32)
    return jnp.sum(hits * places[None, :], axis=1)


def body(
    suffix_query,
    suffix_key_value,
    suffix_resid,
    decode_query_rows,
    decode_key_value,
    decode_resid,
    out_weight,
    post_gain,
    prefix_page_store,
    prefix_table,
    decode_page_store,
    page_table,
    suffix_lengths,
    suffix_prefix,
    decode_ages,
):
    head_dim = HEAD_SIZE
    page_len = PAGE_TOKENS
    q_scale = (D // QUERY_HEADS) ** (-0.5)
    tok_rows = suffix_query.shape[0]
    q_heads = suffix_query.shape[1] // head_dim
    kv_heads = suffix_key_value.shape[2] // head_dim
    query_group_width = q_heads // kv_heads
    blk_size = lax.axis_size("blk")
    my_index = lax.axis_index("blk")

    local_pages = prefix_page_store.shape[1]
    dq_rows = decode_query_rows.shape[0]
    kv_width = kv_heads * head_dim
    dq_lines = decode_query_rows.size // kv_width
    dkv_lines = decode_key_value.size // kv_width
    dec_local = jnp.concatenate(
        [
            decode_query_rows.reshape(dq_lines, kv_width),
            decode_key_value.reshape(dkv_lines, kv_width),
        ],
        axis=0,
    )
    dec_all = lax.all_to_all(
        jnp.broadcast_to(dec_local[None], (blk_size,) + dec_local.shape), "blk", 0, 0, tiled=False
    )
    all_dq = dec_all[:, :dq_lines].reshape(blk_size * dq_rows, q_heads * head_dim)
    all_dkv = (
        dec_all[:, dq_lines:]
        .reshape(blk_size, 2, dq_rows, kv_width)
        .transpose(1, 0, 2, 3)
        .reshape(2, blk_size * dq_rows, kv_width)
    )

    held_rows = local_pages * page_len
    piece = prefix_page_store.reshape(2, held_rows, kv_heads, head_dim).transpose(0, 2, 1, 3)
    gathered = lax.all_gather(piece, "blk", axis=0, tiled=False)

    look_back = 4
    pieces_back = [from_behind(suffix_key_value, "blk", d) for d in range(look_back, 0, -1)]
    window = jnp.concatenate(pieces_back + [suffix_key_value], axis=1)

    kv_size = lax.axis_size("kv")
    out_cols = out_weight.shape[1] // kv_size
    weight_blocks = out_weight.reshape(out_weight.shape[0], kv_size, out_cols).transpose(1, 0, 2)
    weight_blocks, window = lax.optimization_barrier((weight_blocks, window))
    my_weight = lax.all_to_all(weight_blocks, "kv", 0, 0, tiled=False)

    own_queries = suffix_query.reshape(tok_rows, kv_heads, query_group_width, head_dim)
    token_ids = my_index * tok_rows + jnp.arange(tok_rows, dtype=jnp.int32)
    tok_start, tok_prefix = token_tables(suffix_lengths, suffix_prefix, token_ids)
    key_ids = (my_index - look_back) * tok_rows + jnp.arange(
        (look_back + 1) * tok_rows, dtype=jnp.int32
    )
    visible = (key_ids[None, :] >= tok_start[:, None]) & (key_ids[None, :] <= token_ids[:, None])
    window_keys = window[0].reshape((look_back + 1) * tok_rows, kv_heads, head_dim)
    window_values = window[1].reshape((look_back + 1) * tok_rows, kv_heads, head_dim)
    own_numer, own_denom = attend(
        own_queries, window_keys, window_values, visible[:, None, None, :], q_scale
    )

    pool_pages = prefix_table.shape[0]
    per_prefix = PREFIX_LENGTH // PAGE_TOKENS
    page_owner = inverse_rows(prefix_table, jnp.arange(pool_pages, dtype=jnp.int32)) // per_prefix
    key_owner = jnp.repeat(page_owner, page_len).reshape(blk_size, 1, held_rows)
    row_prefix = jnp.repeat(tok_prefix, query_group_width)[:, None]
    rows_q = tok_rows * query_group_width
    q_by_head = own_queries.transpose(1, 0, 2, 3).reshape(kv_heads, rows_q, head_dim)
    numer_p, denom_p = prefix_attention(q_by_head, gathered, key_owner, row_prefix, q_scale)
    pre_numer = numer_p.reshape(kv_heads, tok_rows, query_group_width, head_dim).transpose(
        1, 0, 2, 3
    )
    pre_denom = denom_p.reshape(kv_heads, tok_rows, query_group_width).transpose(1, 0, 2)
    suffix_attn = ((own_numer + pre_numer) / (own_denom + pre_denom)[..., None]).astype(
        jnp.bfloat16
    )
    suffix_attn = suffix_attn.reshape(tok_rows, q_heads * head_dim)

    slot_total = all_dq.shape[0]
    slot_pages = SLOT_CAPACITY // PAGE_TOKENS
    local_cache = decode_page_store.shape[1]
    page_ids = my_index * local_cache + jnp.arange(local_cache, dtype=jnp.int32)
    position = inverse_rows(page_table, page_ids)
    slot_of = position // slot_pages
    block_of = position % slot_pages
    slot_hot = slot_of[:, None] == jnp.arange(slot_total, dtype=jnp.int32)[None, :]
    page_age = jnp.sum(slot_hot.astype(jnp.int32) * decode_ages[None, :], axis=1)
    select = slot_hot.astype(jnp.bfloat16)
    new_rows = jnp.einsum(
        "ls,tsc->tlc", select, all_dkv, preferred_element_type=jnp.float32
    ).astype(jnp.bfloat16)
    write_here = (block_of == page_age // page_len)[:, None] & (
        jnp.arange(page_len, dtype=jnp.int32)[None, :] == (page_age % page_len)[:, None]
    )
    new_cache = jnp.where(write_here[None, :, :, None], new_rows[:, :, None, :], decode_page_store)
    page_queries = jnp.dot(select, all_dq, preferred_element_type=jnp.float32).astype(jnp.bfloat16)
    page_queries = page_queries.reshape(local_cache, kv_heads, query_group_width, head_dim)
    key_cache = new_cache[0].reshape(local_cache, page_len, kv_heads, head_dim)
    value_cache = new_cache[1].reshape(local_cache, page_len, kv_heads, head_dim)
    logits = (
        jnp.einsum("lhgd,lphd->lhgp", page_queries, key_cache, preferred_element_type=jnp.float32)
        * q_scale
    )
    capped = soft_cap * jnp.tanh(logits / soft_cap)
    places = block_of[:, None] * page_len + jnp.arange(page_len, dtype=jnp.int32)[None, :]
    seen_pos = places <= page_age[:, None]
    weights = jnp.where(seen_pos[:, None, None, :], jnp.exp(capped), 0.0)
    page_denom = jnp.sum(weights, axis=3)
    page_numer = jnp.einsum(
        "lhgp,lphd->lhgd",
        weights.astype(jnp.bfloat16),
        value_cache,
        preferred_element_type=jnp.float32,
    )
    slot_float = slot_hot.astype(jnp.float32)
    page_sums = jnp.concatenate([page_numer, page_denom[..., None]], axis=3)
    slot_sums = jnp.einsum("ls,lhgd->shgd", slot_float, page_sums, precision=lax.Precision.HIGHEST)
    slot_sums = slot_sums.reshape((blk_size, slot_total // blk_size) + slot_sums.shape[1:])
    mine_sums = jnp.sum(lax.all_to_all(slot_sums, "blk", 0, 0, tiled=False), axis=0)
    mine_numer = mine_sums[..., :head_dim]
    mine_denom = mine_sums[..., head_dim]
    decode_attn = (mine_numer / mine_denom[..., None]).astype(jnp.bfloat16)
    decode_rows = decode_attn.shape[0]
    decode_attn = decode_attn.reshape(decode_rows, q_heads * head_dim)

    attention = jnp.concatenate([suffix_attn, decode_attn], axis=0)
    kv_size = lax.axis_size("kv")
    residual = jnp.concatenate([suffix_resid, decode_resid], axis=0).astype(jnp.float32)
    heard = lax.all_to_all(
        jnp.broadcast_to(attention[None], (kv_size,) + attention.shape), "kv", 0, 0, tiled=False
    )
    mine = jnp.einsum("srk,sko->ro", heard, my_weight, preferred_element_type=jnp.float32)
    squares = jnp.sum(mine * mine, axis=1)
    square_parts = lax.all_to_all(
        jnp.broadcast_to(squares[None], (kv_size,) + squares.shape), "kv", 0, 0, tiled=False
    )
    mean_square = jnp.sum(square_parts, axis=0) / D
    normed = mine * lax.rsqrt(mean_square + norm_eps)[:, None] * post_gain[None, :]
    hidden = (residual + normed).astype(jnp.bfloat16)
    return (hidden[:tok_rows], hidden[tok_rows:], new_cache)


def solution(mesh):
    placed = (
        P("blk", "kv"),
        P(None, "blk", "kv"),
        P("blk", "kv"),
        P("blk", "kv"),
        P(None, "blk", "kv"),
        P("blk", "kv"),
        P("kv", None),
        P("kv"),
        P(None, "blk", None, "kv"),
        P(),
        P(None, "blk", None, "kv"),
        P(),
        P(),
        P(),
        P(),
    )
    return jax.shard_map(
        body,
        mesh=mesh,
        in_specs=placed,
        out_specs=(P("blk", "kv"), P("blk", "kv"), P(None, "blk", None, "kv")),
        check_vma=False,
    )
```

```python
import functools
import math

import jax
import jax.numpy as jnp
from jax import lax
from jax.experimental import pallas as pl
from jax.experimental.pallas import tpu as pltpu
from jax.sharding import PartitionSpec as P

D = 4608
QUERY_HEADS = 32
HEAD_SIZE = 128
PAGE_TOKENS = 128
PREFIX_LENGTH = 3072
SLOT_CAPACITY = 1024


soft_cap = 50.0
norm_eps = 1e-06


def prefix_kernel(q_ref, k_ref, v_ref, own_ref, row_ref, num_ref, den_ref, *, q_scale, group):
    step = pl.program_id(1)

    @pl.when(step == 0)
    def _():
        num_ref[...] = jnp.zeros_like(num_ref)
        den_ref[...] = jnp.zeros_like(den_ref)

    q = q_ref[0]
    rows = row_ref[...]
    numer = num_ref[0]
    denom = den_ref[0]
    for part in range(group):
        k = k_ref[part, 0, 0]
        v = v_ref[part, 0, 0]
        s = lax.dot_general(q, k, (((1,), (1,)), ((), ())), preferred_element_type=jnp.float32)
        capped = soft_cap * jnp.tanh(s * (q_scale / soft_cap))
        seen = rows == own_ref[part]
        w = jnp.where(seen, jnp.exp(capped), 0.0)
        denom = denom + jnp.sum(w, axis=1, keepdims=True)
        numer = numer + jnp.dot(w.astype(jnp.bfloat16), v, preferred_element_type=jnp.float32)
    num_ref[0] = numer
    den_ref[0] = denom


def prefix_attention(q_heads, gathered, key_owner, row_prefix, q_scale, group=8):
    heads, rows_q, head_dim = q_heads.shape
    sources, _, _, held_rows, _ = gathered.shape
    steps = sources // group
    kern = functools.partial(prefix_kernel, q_scale=q_scale, group=group)
    return pl.pallas_call(
        kern,
        grid=(heads, steps),
        in_specs=[
            pl.BlockSpec((1, rows_q, head_dim), lambda h, j: (h, 0, 0)),
            pl.BlockSpec((group, 1, 1, held_rows, head_dim), lambda h, j: (j, 0, h, 0, 0)),
            pl.BlockSpec((group, 1, 1, held_rows, head_dim), lambda h, j: (j, 1, h, 0, 0)),
            pl.BlockSpec((group, 1, held_rows), lambda h, j: (j, 0, 0)),
            pl.BlockSpec((rows_q, 1), lambda h, j: (0, 0)),
        ],
        out_specs=[
            pl.BlockSpec((1, rows_q, head_dim), lambda h, j: (h, 0, 0)),
            pl.BlockSpec((1, rows_q, 1), lambda h, j: (h, 0, 0)),
        ],
        out_shape=[
            jax.ShapeDtypeStruct((heads, rows_q, head_dim), jnp.float32),
            jax.ShapeDtypeStruct((heads, rows_q, 1), jnp.float32),
        ],
        compiler_params=pltpu.CompilerParams(dimension_semantics=("parallel", "arbitrary")),
    )(q_heads, gathered, gathered, key_owner, row_prefix)


def from_behind(block, axis, distance):
    devices = range(lax.axis_size(axis))
    route = [(i - distance, i) for i in devices if i - distance in devices]
    return lax.ppermute(block, axis, route)


def attend(query_rows, key_rows, value_rows, visible, q_scale):
    logits = (
        jnp.einsum("qhgd,khd->qhgk", query_rows, key_rows, preferred_element_type=jnp.float32)
        * q_scale
    )
    capped = soft_cap * jnp.tanh(logits / soft_cap)
    weights = jnp.where(visible, jnp.exp(capped), 0.0)
    denominator = jnp.sum(weights, axis=3)
    numerator = jnp.einsum(
        "qhgk,khd->qhgd",
        weights.astype(jnp.bfloat16),
        value_rows,
        preferred_element_type=jnp.float32,
    )
    return (numerator, denominator)


def token_tables(lengths, prefix_ids, token_ids):
    suffix_ends = jnp.cumsum(lengths)
    starts = suffix_ends - lengths
    inside = (
        (token_ids[:, None] >= starts[None, :]) & (token_ids[:, None] < suffix_ends[None, :])
    ).astype(jnp.int32)
    tok_start = jnp.sum(inside * starts[None, :], axis=1)
    tok_prefix = jnp.sum(inside * prefix_ids[None, :], axis=1)
    return (tok_start, tok_prefix)


def inverse_rows(table, wanted):
    hits = (table[None, :] == wanted[:, None]).astype(jnp.int32)
    places = jnp.arange(table.shape[0], dtype=jnp.int32)
    return jnp.sum(hits * places[None, :], axis=1)


def body(
    suffix_query,
    suffix_key_value,
    suffix_resid,
    decode_query_rows,
    decode_key_value,
    decode_resid,
    out_weight,
    post_gain,
    prefix_page_store,
    prefix_table,
    decode_page_store,
    page_table,
    suffix_lengths,
    suffix_prefix,
    decode_ages,
):
    head_dim = HEAD_SIZE
    page_len = PAGE_TOKENS
    q_scale = (D // QUERY_HEADS) ** (-0.5)
    tok_rows = suffix_query.shape[0]
    q_heads = suffix_query.shape[1] // head_dim
    kv_heads = suffix_key_value.shape[2] // head_dim
    query_group_width = q_heads // kv_heads
    blk_size = lax.axis_size("blk")
    my_index = lax.axis_index("blk")

    local_pages = prefix_page_store.shape[1]
    dq_rows = decode_query_rows.shape[0]
    kv_width = kv_heads * head_dim
    dq_lines = decode_query_rows.size // kv_width
    dkv_lines = decode_key_value.size // kv_width
    dec_local = jnp.concatenate(
        [
            decode_query_rows.reshape(dq_lines, kv_width),
            decode_key_value.reshape(dkv_lines, kv_width),
        ],
        axis=0,
    )
    dec_all = lax.all_to_all(
        jnp.broadcast_to(dec_local[None], (blk_size,) + dec_local.shape), "blk", 0, 0, tiled=False
    )
    all_dq = dec_all[:, :dq_lines].reshape(blk_size * dq_rows, q_heads * head_dim)
    all_dkv = (
        dec_all[:, dq_lines:]
        .reshape(blk_size, 2, dq_rows, kv_width)
        .transpose(1, 0, 2, 3)
        .reshape(2, blk_size * dq_rows, kv_width)
    )

    held_rows = local_pages * page_len
    piece = prefix_page_store.reshape(2, held_rows, kv_heads, head_dim).transpose(0, 2, 1, 3)
    gathered = lax.all_gather(piece, "blk", axis=0, tiled=False)

    look_back = 4
    pieces_back = [from_behind(suffix_key_value, "blk", d) for d in range(look_back, 0, -1)]
    window = jnp.concatenate(pieces_back + [suffix_key_value], axis=1)

    own_queries = suffix_query.reshape(tok_rows, kv_heads, query_group_width, head_dim)
    token_ids = my_index * tok_rows + jnp.arange(tok_rows, dtype=jnp.int32)
    tok_start, tok_prefix = token_tables(suffix_lengths, suffix_prefix, token_ids)
    key_ids = (my_index - look_back) * tok_rows + jnp.arange(
        (look_back + 1) * tok_rows, dtype=jnp.int32
    )
    visible = (key_ids[None, :] >= tok_start[:, None]) & (key_ids[None, :] <= token_ids[:, None])
    window_keys = window[0].reshape((look_back + 1) * tok_rows, kv_heads, head_dim)
    window_values = window[1].reshape((look_back + 1) * tok_rows, kv_heads, head_dim)
    own_numer, own_denom = attend(
        own_queries, window_keys, window_values, visible[:, None, None, :], q_scale
    )

    pool_pages = prefix_table.shape[0]
    per_prefix = PREFIX_LENGTH // PAGE_TOKENS
    page_owner = inverse_rows(prefix_table, jnp.arange(pool_pages, dtype=jnp.int32)) // per_prefix
    key_owner = jnp.repeat(page_owner, page_len).reshape(blk_size, 1, held_rows)
    row_prefix = jnp.repeat(tok_prefix, query_group_width)[:, None]
    rows_q = tok_rows * query_group_width
    q_by_head = own_queries.transpose(1, 0, 2, 3).reshape(kv_heads, rows_q, head_dim)
    numer_p, denom_p = prefix_attention(q_by_head, gathered, key_owner, row_prefix, q_scale)
    pre_numer = numer_p.reshape(kv_heads, tok_rows, query_group_width, head_dim).transpose(
        1, 0, 2, 3
    )
    pre_denom = denom_p.reshape(kv_heads, tok_rows, query_group_width).transpose(1, 0, 2)
    suffix_attn = ((own_numer + pre_numer) / (own_denom + pre_denom)[..., None]).astype(
        jnp.bfloat16
    )
    suffix_attn = suffix_attn.reshape(tok_rows, q_heads * head_dim)

    slot_total = all_dq.shape[0]
    slot_pages = SLOT_CAPACITY // PAGE_TOKENS
    local_cache = decode_page_store.shape[1]
    page_ids = my_index * local_cache + jnp.arange(local_cache, dtype=jnp.int32)
    position = inverse_rows(page_table, page_ids)
    slot_of = position // slot_pages
    block_of = position % slot_pages
    slot_hot = slot_of[:, None] == jnp.arange(slot_total, dtype=jnp.int32)[None, :]
    page_age = jnp.sum(slot_hot.astype(jnp.int32) * decode_ages[None, :], axis=1)
    select = slot_hot.astype(jnp.bfloat16)
    new_rows = jnp.einsum(
        "ls,tsc->tlc", select, all_dkv, preferred_element_type=jnp.float32
    ).astype(jnp.bfloat16)
    write_here = (block_of == page_age // page_len)[:, None] & (
        jnp.arange(page_len, dtype=jnp.int32)[None, :] == (page_age % page_len)[:, None]
    )
    new_cache = jnp.where(write_here[None, :, :, None], new_rows[:, :, None, :], decode_page_store)
    page_queries = jnp.dot(select, all_dq, preferred_element_type=jnp.float32).astype(jnp.bfloat16)
    page_queries = page_queries.reshape(local_cache, kv_heads, query_group_width, head_dim)
    key_cache = new_cache[0].reshape(local_cache, page_len, kv_heads, head_dim)
    value_cache = new_cache[1].reshape(local_cache, page_len, kv_heads, head_dim)
    logits = (
        jnp.einsum("lhgd,lphd->lhgp", page_queries, key_cache, preferred_element_type=jnp.float32)
        * q_scale
    )
    capped = soft_cap * jnp.tanh(logits / soft_cap)
    places = block_of[:, None] * page_len + jnp.arange(page_len, dtype=jnp.int32)[None, :]
    seen_pos = places <= page_age[:, None]
    weights = jnp.where(seen_pos[:, None, None, :], jnp.exp(capped), 0.0)
    page_denom = jnp.sum(weights, axis=3)
    page_numer = jnp.einsum(
        "lhgp,lphd->lhgd",
        weights.astype(jnp.bfloat16),
        value_cache,
        preferred_element_type=jnp.float32,
    )
    slot_float = slot_hot.astype(jnp.float32)
    page_sums = jnp.concatenate([page_numer, page_denom[..., None]], axis=3)
    slot_sums = jnp.einsum("ls,lhgd->shgd", slot_float, page_sums, precision=lax.Precision.HIGHEST)
    slot_sums = slot_sums.reshape((blk_size, slot_total // blk_size) + slot_sums.shape[1:])
    mine_sums = jnp.sum(lax.all_to_all(slot_sums, "blk", 0, 0, tiled=False), axis=0)
    mine_numer = mine_sums[..., :head_dim]
    mine_denom = mine_sums[..., head_dim]
    decode_attn = (mine_numer / mine_denom[..., None]).astype(jnp.bfloat16)
    decode_rows = decode_attn.shape[0]
    decode_attn = decode_attn.reshape(decode_rows, q_heads * head_dim)

    attention = jnp.concatenate([suffix_attn, decode_attn], axis=0)
    kv_size = lax.axis_size("kv")
    weight_blocks = out_weight.reshape(out_weight.shape[0], kv_size, -1)
    shares = jnp.einsum(
        "rk,kdo->dro", attention, weight_blocks, preferred_element_type=jnp.float32
    ).astype(jnp.bfloat16)
    residual = jnp.concatenate([suffix_resid, decode_resid], axis=0).astype(jnp.float32)
    mine = jnp.sum(lax.all_to_all(shares, "kv", 0, 0, tiled=False).astype(jnp.float32), axis=0)
    squares = jnp.sum(mine * mine, axis=1)
    square_parts = lax.all_to_all(
        jnp.broadcast_to(squares[None], (kv_size,) + squares.shape), "kv", 0, 0, tiled=False
    )
    mean_square = jnp.sum(square_parts, axis=0) / D
    normed = mine * lax.rsqrt(mean_square + norm_eps)[:, None] * post_gain[None, :]
    hidden = (residual + normed).astype(jnp.bfloat16)
    return (hidden[:tok_rows], hidden[tok_rows:], new_cache)


def solution(mesh):
    placed = (
        P("blk", "kv"),
        P(None, "blk", "kv"),
        P("blk", "kv"),
        P("blk", "kv"),
        P(None, "blk", "kv"),
        P("blk", "kv"),
        P("kv", None),
        P("kv"),
        P(None, "blk", None, "kv"),
        P(),
        P(None, "blk", None, "kv"),
        P(),
        P(),
        P(),
        P(),
    )
    return jax.shard_map(
        body,
        mesh=mesh,
        in_specs=placed,
        out_specs=(P("blk", "kv"), P("blk", "kv"), P(None, "blk", None, "kv")),
        check_vma=False,
    )
```

```python
import functools
import math

import jax
import jax.numpy as jnp
from jax import lax
from jax.experimental import pallas as pl
from jax.experimental.pallas import tpu as pltpu
from jax.sharding import PartitionSpec as P

D = 4608
QUERY_HEADS = 32
HEAD_SIZE = 128
PAGE_TOKENS = 128
PREFIX_LENGTH = 3072
SLOT_CAPACITY = 1024


soft_cap = 50.0
norm_eps = 1e-06


def prefix_kernel(q_ref, k_ref, v_ref, own_ref, row_ref, num_ref, den_ref, *, q_scale, group):
    step = pl.program_id(1)

    @pl.when(step == 0)
    def _():
        num_ref[...] = jnp.zeros_like(num_ref)
        den_ref[...] = jnp.zeros_like(den_ref)

    q = q_ref[0]
    rows = row_ref[...]
    numer = num_ref[0]
    denom = den_ref[0]
    for part in range(group):
        k = k_ref[part, 0, 0]
        v = v_ref[part, 0, 0]
        s = lax.dot_general(q, k, (((1,), (1,)), ((), ())), preferred_element_type=jnp.float32)
        capped = soft_cap * jnp.tanh(s * (q_scale / soft_cap))
        seen = rows == own_ref[part]
        w = jnp.where(seen, jnp.exp(capped), 0.0)
        denom = denom + jnp.sum(w, axis=1, keepdims=True)
        numer = numer + jnp.dot(w.astype(jnp.bfloat16), v, preferred_element_type=jnp.float32)
    num_ref[0] = numer
    den_ref[0] = denom


def prefix_attention(q_heads, gathered, key_owner, row_prefix, q_scale, group=16):
    heads, rows_q, head_dim = q_heads.shape
    sources, _, _, held_rows, _ = gathered.shape
    steps = sources // group
    kern = functools.partial(prefix_kernel, q_scale=q_scale, group=group)
    return pl.pallas_call(
        kern,
        grid=(heads, steps),
        in_specs=[
            pl.BlockSpec((1, rows_q, head_dim), lambda h, j: (h, 0, 0)),
            pl.BlockSpec((group, 1, 1, held_rows, head_dim), lambda h, j: (j, 0, h, 0, 0)),
            pl.BlockSpec((group, 1, 1, held_rows, head_dim), lambda h, j: (j, 1, h, 0, 0)),
            pl.BlockSpec((group, 1, held_rows), lambda h, j: (j, 0, 0)),
            pl.BlockSpec((rows_q, 1), lambda h, j: (0, 0)),
        ],
        out_specs=[
            pl.BlockSpec((1, rows_q, head_dim), lambda h, j: (h, 0, 0)),
            pl.BlockSpec((1, rows_q, 1), lambda h, j: (h, 0, 0)),
        ],
        out_shape=[
            jax.ShapeDtypeStruct((heads, rows_q, head_dim), jnp.float32),
            jax.ShapeDtypeStruct((heads, rows_q, 1), jnp.float32),
        ],
        compiler_params=pltpu.CompilerParams(dimension_semantics=("parallel", "arbitrary")),
    )(q_heads, gathered, gathered, key_owner, row_prefix)


def from_behind(block, axis, distance):
    devices = range(lax.axis_size(axis))
    route = [(i - distance, i) for i in devices if i - distance in devices]
    return lax.ppermute(block, axis, route)


def attend(query_rows, key_rows, value_rows, visible, q_scale):
    logits = (
        jnp.einsum("qhgd,khd->qhgk", query_rows, key_rows, preferred_element_type=jnp.float32)
        * q_scale
    )
    capped = soft_cap * jnp.tanh(logits / soft_cap)
    weights = jnp.where(visible, jnp.exp(capped), 0.0)
    denominator = jnp.sum(weights, axis=3)
    numerator = jnp.einsum(
        "qhgk,khd->qhgd",
        weights.astype(jnp.bfloat16),
        value_rows,
        preferred_element_type=jnp.float32,
    )
    return (numerator, denominator)


def token_tables(lengths, prefix_ids, token_ids):
    suffix_ends = jnp.cumsum(lengths)
    starts = suffix_ends - lengths
    inside = (
        (token_ids[:, None] >= starts[None, :]) & (token_ids[:, None] < suffix_ends[None, :])
    ).astype(jnp.int32)
    tok_start = jnp.sum(inside * starts[None, :], axis=1)
    tok_prefix = jnp.sum(inside * prefix_ids[None, :], axis=1)
    return (tok_start, tok_prefix)


def inverse_rows(table, wanted):
    hits = (table[None, :] == wanted[:, None]).astype(jnp.int32)
    places = jnp.arange(table.shape[0], dtype=jnp.int32)
    return jnp.sum(hits * places[None, :], axis=1)


def body(
    suffix_query,
    suffix_key_value,
    suffix_resid,
    decode_query_rows,
    decode_key_value,
    decode_resid,
    out_weight,
    post_gain,
    prefix_page_store,
    prefix_table,
    decode_page_store,
    page_table,
    suffix_lengths,
    suffix_prefix,
    decode_ages,
):
    head_dim = HEAD_SIZE
    page_len = PAGE_TOKENS
    q_scale = (D // QUERY_HEADS) ** (-0.5)
    tok_rows = suffix_query.shape[0]
    q_heads = suffix_query.shape[1] // head_dim
    kv_heads = suffix_key_value.shape[2] // head_dim
    query_group_width = q_heads // kv_heads
    blk_size = lax.axis_size("blk")
    my_index = lax.axis_index("blk")

    local_pages = prefix_page_store.shape[1]
    dq_rows = decode_query_rows.shape[0]
    kv_width = kv_heads * head_dim
    dq_lines = decode_query_rows.size // kv_width
    dkv_lines = decode_key_value.size // kv_width
    dec_local = jnp.concatenate(
        [
            decode_query_rows.reshape(dq_lines, kv_width),
            decode_key_value.reshape(dkv_lines, kv_width),
        ],
        axis=0,
    )
    dec_all = lax.all_to_all(
        jnp.broadcast_to(dec_local[None], (blk_size,) + dec_local.shape), "blk", 0, 0, tiled=False
    )
    all_dq = dec_all[:, :dq_lines].reshape(blk_size * dq_rows, q_heads * head_dim)
    all_dkv = (
        dec_all[:, dq_lines:]
        .reshape(blk_size, 2, dq_rows, kv_width)
        .transpose(1, 0, 2, 3)
        .reshape(2, blk_size * dq_rows, kv_width)
    )

    held_rows = local_pages * page_len
    piece = prefix_page_store.reshape(2, held_rows, kv_heads, head_dim).transpose(0, 2, 1, 3)
    gathered = lax.all_gather(piece, "blk", axis=0, tiled=False)

    look_back = 4
    pieces_back = [from_behind(suffix_key_value, "blk", d) for d in range(look_back, 0, -1)]
    window = jnp.concatenate(pieces_back + [suffix_key_value], axis=1)

    own_queries = suffix_query.reshape(tok_rows, kv_heads, query_group_width, head_dim)
    token_ids = my_index * tok_rows + jnp.arange(tok_rows, dtype=jnp.int32)
    tok_start, tok_prefix = token_tables(suffix_lengths, suffix_prefix, token_ids)
    key_ids = (my_index - look_back) * tok_rows + jnp.arange(
        (look_back + 1) * tok_rows, dtype=jnp.int32
    )
    visible = (key_ids[None, :] >= tok_start[:, None]) & (key_ids[None, :] <= token_ids[:, None])
    window_keys = window[0].reshape((look_back + 1) * tok_rows, kv_heads, head_dim)
    window_values = window[1].reshape((look_back + 1) * tok_rows, kv_heads, head_dim)
    own_numer, own_denom = attend(
        own_queries, window_keys, window_values, visible[:, None, None, :], q_scale
    )

    pool_pages = prefix_table.shape[0]
    per_prefix = PREFIX_LENGTH // PAGE_TOKENS
    page_owner = inverse_rows(prefix_table, jnp.arange(pool_pages, dtype=jnp.int32)) // per_prefix
    key_owner = jnp.repeat(page_owner, page_len).reshape(blk_size, 1, held_rows)
    row_prefix = jnp.repeat(tok_prefix, query_group_width)[:, None]
    rows_q = tok_rows * query_group_width
    q_by_head = own_queries.transpose(1, 0, 2, 3).reshape(kv_heads, rows_q, head_dim)
    numer_p, denom_p = prefix_attention(q_by_head, gathered, key_owner, row_prefix, q_scale)
    pre_numer = numer_p.reshape(kv_heads, tok_rows, query_group_width, head_dim).transpose(
        1, 0, 2, 3
    )
    pre_denom = denom_p.reshape(kv_heads, tok_rows, query_group_width).transpose(1, 0, 2)
    suffix_attn = ((own_numer + pre_numer) / (own_denom + pre_denom)[..., None]).astype(
        jnp.bfloat16
    )
    suffix_attn = suffix_attn.reshape(tok_rows, q_heads * head_dim)

    slot_total = all_dq.shape[0]
    slot_pages = SLOT_CAPACITY // PAGE_TOKENS
    local_cache = decode_page_store.shape[1]
    page_ids = my_index * local_cache + jnp.arange(local_cache, dtype=jnp.int32)
    position = inverse_rows(page_table, page_ids)
    slot_of = position // slot_pages
    block_of = position % slot_pages
    slot_hot = slot_of[:, None] == jnp.arange(slot_total, dtype=jnp.int32)[None, :]
    page_age = jnp.sum(slot_hot.astype(jnp.int32) * decode_ages[None, :], axis=1)
    select = slot_hot.astype(jnp.bfloat16)
    new_rows = jnp.einsum(
        "ls,tsc->tlc", select, all_dkv, preferred_element_type=jnp.float32
    ).astype(jnp.bfloat16)
    write_here = (block_of == page_age // page_len)[:, None] & (
        jnp.arange(page_len, dtype=jnp.int32)[None, :] == (page_age % page_len)[:, None]
    )
    new_cache = jnp.where(write_here[None, :, :, None], new_rows[:, :, None, :], decode_page_store)
    page_queries = jnp.dot(select, all_dq, preferred_element_type=jnp.float32).astype(jnp.bfloat16)
    page_queries = page_queries.reshape(local_cache, kv_heads, query_group_width, head_dim)
    key_cache = new_cache[0].reshape(local_cache, page_len, kv_heads, head_dim)
    value_cache = new_cache[1].reshape(local_cache, page_len, kv_heads, head_dim)
    logits = (
        jnp.einsum("lhgd,lphd->lhgp", page_queries, key_cache, preferred_element_type=jnp.float32)
        * q_scale
    )
    capped = soft_cap * jnp.tanh(logits / soft_cap)
    places = block_of[:, None] * page_len + jnp.arange(page_len, dtype=jnp.int32)[None, :]
    seen_pos = places <= page_age[:, None]
    weights = jnp.where(seen_pos[:, None, None, :], jnp.exp(capped), 0.0)
    page_denom = jnp.sum(weights, axis=3)
    page_numer = jnp.einsum(
        "lhgp,lphd->lhgd",
        weights.astype(jnp.bfloat16),
        value_cache,
        preferred_element_type=jnp.float32,
    )
    slot_float = slot_hot.astype(jnp.float32)
    page_sums = jnp.concatenate([page_numer, page_denom[..., None]], axis=3)
    slot_sums = jnp.einsum("ls,lhgd->shgd", slot_float, page_sums, precision=lax.Precision.HIGHEST)
    slot_sums = slot_sums.reshape((blk_size, slot_total // blk_size) + slot_sums.shape[1:])
    mine_sums = jnp.sum(lax.all_to_all(slot_sums, "blk", 0, 0, tiled=False), axis=0)
    mine_numer = mine_sums[..., :head_dim]
    mine_denom = mine_sums[..., head_dim]
    decode_attn = (mine_numer / mine_denom[..., None]).astype(jnp.bfloat16)
    decode_rows = decode_attn.shape[0]
    decode_attn = decode_attn.reshape(decode_rows, q_heads * head_dim)

    attention = jnp.concatenate([suffix_attn, decode_attn], axis=0)
    kv_size = lax.axis_size("kv")
    weight_blocks = out_weight.reshape(out_weight.shape[0], kv_size, -1)
    shares = jnp.einsum(
        "rk,kdo->dro", attention, weight_blocks, preferred_element_type=jnp.float32
    ).astype(jnp.bfloat16)
    residual = jnp.concatenate([suffix_resid, decode_resid], axis=0).astype(jnp.float32)
    mine = jnp.sum(lax.all_to_all(shares, "kv", 0, 0, tiled=False).astype(jnp.float32), axis=0)
    squares = jnp.sum(mine * mine, axis=1)
    square_parts = lax.all_to_all(
        jnp.broadcast_to(squares[None], (kv_size,) + squares.shape), "kv", 0, 0, tiled=False
    )
    mean_square = jnp.sum(square_parts, axis=0) / D
    normed = mine * lax.rsqrt(mean_square + norm_eps)[:, None] * post_gain[None, :]
    hidden = (residual + normed).astype(jnp.bfloat16)
    return (hidden[:tok_rows], hidden[tok_rows:], new_cache)


def solution(mesh):
    placed = (
        P("blk", "kv"),
        P(None, "blk", "kv"),
        P("blk", "kv"),
        P("blk", "kv"),
        P(None, "blk", "kv"),
        P("blk", "kv"),
        P("kv", None),
        P("kv"),
        P(None, "blk", None, "kv"),
        P(),
        P(None, "blk", None, "kv"),
        P(),
        P(),
        P(),
        P(),
    )
    return jax.shard_map(
        body,
        mesh=mesh,
        in_specs=placed,
        out_specs=(P("blk", "kv"), P("blk", "kv"), P(None, "blk", None, "kv")),
        check_vma=False,
    )
```

```python
import functools
import math

import jax
import jax.numpy as jnp
from jax import lax
from jax.experimental import pallas as pl
from jax.experimental.pallas import tpu as pltpu
from jax.sharding import PartitionSpec as P

D = 4608
QUERY_HEADS = 32
HEAD_SIZE = 128
PAGE_TOKENS = 128
PREFIX_LENGTH = 3072
SLOT_CAPACITY = 1024


soft_cap = 50.0
norm_eps = 1e-06


def prefix_kernel(q_ref, k_ref, v_ref, own_ref, row_ref, num_ref, den_ref, *, q_scale, group):
    step = pl.program_id(1)

    @pl.when(step == 0)
    def _():
        num_ref[...] = jnp.zeros_like(num_ref)
        den_ref[...] = jnp.zeros_like(den_ref)

    q = q_ref[0]
    rows = row_ref[...]
    numer = num_ref[0]
    denom = den_ref[0]
    for part in range(group):
        k = k_ref[part, 0, 0]
        v = v_ref[part, 0, 0]
        s = lax.dot_general(q, k, (((1,), (1,)), ((), ())), preferred_element_type=jnp.float32)
        capped = soft_cap * jnp.tanh(s * (q_scale / soft_cap))
        seen = rows == own_ref[part]
        w = jnp.where(seen, jnp.exp(capped), 0.0)
        denom = denom + jnp.sum(w, axis=1, keepdims=True)
        numer = numer + jnp.dot(w.astype(jnp.bfloat16), v, preferred_element_type=jnp.float32)
    num_ref[0] = numer
    den_ref[0] = denom


def prefix_attention(q_heads, gathered, key_owner, row_prefix, q_scale, group=16):
    heads, rows_q, head_dim = q_heads.shape
    sources, _, _, held_rows, _ = gathered.shape
    steps = sources // group
    kern = functools.partial(prefix_kernel, q_scale=q_scale, group=group)
    return pl.pallas_call(
        kern,
        grid=(heads, steps),
        in_specs=[
            pl.BlockSpec((1, rows_q, head_dim), lambda h, j: (h, 0, 0)),
            pl.BlockSpec((group, 1, 1, held_rows, head_dim), lambda h, j: (j, 0, h, 0, 0)),
            pl.BlockSpec((group, 1, 1, held_rows, head_dim), lambda h, j: (j, 1, h, 0, 0)),
            pl.BlockSpec((group, 1, held_rows), lambda h, j: (j, 0, 0)),
            pl.BlockSpec((rows_q, 1), lambda h, j: (0, 0)),
        ],
        out_specs=[
            pl.BlockSpec((1, rows_q, head_dim), lambda h, j: (h, 0, 0)),
            pl.BlockSpec((1, rows_q, 1), lambda h, j: (h, 0, 0)),
        ],
        out_shape=[
            jax.ShapeDtypeStruct((heads, rows_q, head_dim), jnp.float32),
            jax.ShapeDtypeStruct((heads, rows_q, 1), jnp.float32),
        ],
        compiler_params=pltpu.CompilerParams(dimension_semantics=("parallel", "arbitrary")),
    )(q_heads, gathered, gathered, key_owner, row_prefix)


def from_behind(block, axis, distance):
    devices = range(lax.axis_size(axis))
    route = [(i - distance, i) for i in devices if i - distance in devices]
    return lax.ppermute(block, axis, route)


def attend(query_rows, key_rows, value_rows, visible, q_scale):
    logits = (
        jnp.einsum("qhgd,khd->qhgk", query_rows, key_rows, preferred_element_type=jnp.float32)
        * q_scale
    )
    capped = soft_cap * jnp.tanh(logits / soft_cap)
    weights = jnp.where(visible, jnp.exp(capped), 0.0)
    denominator = jnp.sum(weights, axis=3)
    numerator = jnp.einsum(
        "qhgk,khd->qhgd",
        weights.astype(jnp.bfloat16),
        value_rows,
        preferred_element_type=jnp.float32,
    )
    return (numerator, denominator)


def token_tables(lengths, prefix_ids, token_ids):
    suffix_ends = jnp.cumsum(lengths)
    starts = suffix_ends - lengths
    inside = (
        (token_ids[:, None] >= starts[None, :]) & (token_ids[:, None] < suffix_ends[None, :])
    ).astype(jnp.int32)
    tok_start = jnp.sum(inside * starts[None, :], axis=1)
    tok_prefix = jnp.sum(inside * prefix_ids[None, :], axis=1)
    return (tok_start, tok_prefix)


def inverse_rows(table, wanted):
    hits = (table[None, :] == wanted[:, None]).astype(jnp.int32)
    places = jnp.arange(table.shape[0], dtype=jnp.int32)
    return jnp.sum(hits * places[None, :], axis=1)


def body(
    suffix_query,
    suffix_key_value,
    suffix_resid,
    decode_query_rows,
    decode_key_value,
    decode_resid,
    out_weight,
    post_gain,
    prefix_page_store,
    prefix_table,
    decode_page_store,
    page_table,
    suffix_lengths,
    suffix_prefix,
    decode_ages,
):
    head_dim = HEAD_SIZE
    page_len = PAGE_TOKENS
    q_scale = (D // QUERY_HEADS) ** (-0.5)
    tok_rows = suffix_query.shape[0]
    q_heads = suffix_query.shape[1] // head_dim
    kv_heads = suffix_key_value.shape[2] // head_dim
    query_group_width = q_heads // kv_heads
    blk_size = lax.axis_size("blk")
    my_index = lax.axis_index("blk")

    local_pages = prefix_page_store.shape[1]
    dq_rows = decode_query_rows.shape[0]
    kv_width = kv_heads * head_dim
    dq_lines = decode_query_rows.size // kv_width
    dkv_lines = decode_key_value.size // kv_width
    dec_local = jnp.concatenate(
        [
            decode_query_rows.reshape(dq_lines, kv_width),
            decode_key_value.reshape(dkv_lines, kv_width),
        ],
        axis=0,
    )
    dec_all = lax.all_to_all(
        jnp.broadcast_to(dec_local[None], (blk_size,) + dec_local.shape), "blk", 0, 0, tiled=False
    )
    all_dq = dec_all[:, :dq_lines].reshape(blk_size * dq_rows, q_heads * head_dim)
    all_dkv = (
        dec_all[:, dq_lines:]
        .reshape(blk_size, 2, dq_rows, kv_width)
        .transpose(1, 0, 2, 3)
        .reshape(2, blk_size * dq_rows, kv_width)
    )

    held_rows = local_pages * page_len
    piece = prefix_page_store.reshape(2, held_rows, kv_heads, head_dim).transpose(0, 2, 1, 3)
    gathered = lax.all_gather(piece, "blk", axis=0, tiled=False)

    look_back = 4
    pieces_back = [from_behind(suffix_key_value, "blk", d) for d in range(look_back, 0, -1)]
    window = jnp.concatenate(pieces_back + [suffix_key_value], axis=1)

    own_queries = suffix_query.reshape(tok_rows, kv_heads, query_group_width, head_dim)
    token_ids = my_index * tok_rows + jnp.arange(tok_rows, dtype=jnp.int32)
    tok_start, tok_prefix = token_tables(suffix_lengths, suffix_prefix, token_ids)
    key_ids = (my_index - look_back) * tok_rows + jnp.arange(
        (look_back + 1) * tok_rows, dtype=jnp.int32
    )
    visible = (key_ids[None, :] >= tok_start[:, None]) & (key_ids[None, :] <= token_ids[:, None])
    window_keys = window[0].reshape((look_back + 1) * tok_rows, kv_heads, head_dim)
    window_values = window[1].reshape((look_back + 1) * tok_rows, kv_heads, head_dim)
    own_numer, own_denom = attend(
        own_queries, window_keys, window_values, visible[:, None, None, :], q_scale
    )

    pool_pages = prefix_table.shape[0]
    per_prefix = PREFIX_LENGTH // PAGE_TOKENS
    page_owner = inverse_rows(prefix_table, jnp.arange(pool_pages, dtype=jnp.int32)) // per_prefix
    key_owner = jnp.repeat(page_owner, page_len).reshape(blk_size, 1, held_rows)
    row_prefix = jnp.repeat(tok_prefix, query_group_width)[:, None]
    rows_q = tok_rows * query_group_width
    q_by_head = own_queries.transpose(1, 0, 2, 3).reshape(kv_heads, rows_q, head_dim)
    numer_p, denom_p = prefix_attention(q_by_head, gathered, key_owner, row_prefix, q_scale)
    pre_numer = numer_p.reshape(kv_heads, tok_rows, query_group_width, head_dim).transpose(
        1, 0, 2, 3
    )
    pre_denom = denom_p.reshape(kv_heads, tok_rows, query_group_width).transpose(1, 0, 2)
    suffix_attn = ((own_numer + pre_numer) / (own_denom + pre_denom)[..., None]).astype(
        jnp.bfloat16
    )
    suffix_attn = suffix_attn.reshape(tok_rows, q_heads * head_dim)

    slot_total = all_dq.shape[0]
    slot_pages = SLOT_CAPACITY // PAGE_TOKENS
    local_cache = decode_page_store.shape[1]
    page_ids = my_index * local_cache + jnp.arange(local_cache, dtype=jnp.int32)
    position = inverse_rows(page_table, page_ids)
    slot_of = position // slot_pages
    block_of = position % slot_pages
    slot_hot = slot_of[:, None] == jnp.arange(slot_total, dtype=jnp.int32)[None, :]
    page_age = jnp.sum(slot_hot.astype(jnp.int32) * decode_ages[None, :], axis=1)
    select = slot_hot.astype(jnp.bfloat16)
    new_rows = jnp.einsum(
        "ls,tsc->tlc", select, all_dkv, preferred_element_type=jnp.float32
    ).astype(jnp.bfloat16)
    write_here = (block_of == page_age // page_len)[:, None] & (
        jnp.arange(page_len, dtype=jnp.int32)[None, :] == (page_age % page_len)[:, None]
    )
    new_cache = jnp.where(write_here[None, :, :, None], new_rows[:, :, None, :], decode_page_store)
    page_queries = jnp.dot(select, all_dq, preferred_element_type=jnp.float32).astype(jnp.bfloat16)
    page_queries = page_queries.reshape(local_cache, kv_heads, query_group_width, head_dim)
    key_cache = new_cache[0].reshape(local_cache, page_len, kv_heads, head_dim)
    value_cache = new_cache[1].reshape(local_cache, page_len, kv_heads, head_dim)
    logits = (
        jnp.einsum("lhgd,lphd->lhgp", page_queries, key_cache, preferred_element_type=jnp.float32)
        * q_scale
    )
    capped = soft_cap * jnp.tanh(logits / soft_cap)
    places = block_of[:, None] * page_len + jnp.arange(page_len, dtype=jnp.int32)[None, :]
    seen_pos = places <= page_age[:, None]
    weights = jnp.where(seen_pos[:, None, None, :], jnp.exp(capped), 0.0)
    page_denom = jnp.sum(weights, axis=3)
    page_numer = jnp.einsum(
        "lhgp,lphd->lhgd",
        weights.astype(jnp.bfloat16),
        value_cache,
        preferred_element_type=jnp.float32,
    )
    slot_float = slot_hot.astype(jnp.float32)
    page_sums = jnp.concatenate([page_numer, page_denom[..., None]], axis=3)
    slot_sums = jnp.einsum("ls,lhgd->shgd", slot_float, page_sums, precision=lax.Precision.HIGHEST)
    slot_sums = slot_sums.reshape((blk_size, slot_total // blk_size) + slot_sums.shape[1:])
    mine_sums = jnp.sum(lax.all_to_all(slot_sums, "blk", 0, 0, tiled=False), axis=0)
    mine_numer = mine_sums[..., :head_dim]
    mine_denom = mine_sums[..., head_dim]
    decode_attn = (mine_numer / mine_denom[..., None]).astype(jnp.bfloat16)
    decode_rows = decode_attn.shape[0]
    decode_attn = decode_attn.reshape(decode_rows, q_heads * head_dim)

    attention = jnp.concatenate([suffix_attn, decode_attn], axis=0)
    kv_size = lax.axis_size("kv")
    weight_blocks = out_weight.reshape(out_weight.shape[0], kv_size, -1)
    shares = jnp.einsum(
        "rk,kdo->dro", attention, weight_blocks, preferred_element_type=jnp.float32
    ).astype(jnp.bfloat16)
    mine = jnp.sum(lax.all_to_all(shares, "kv", 0, 0, tiled=False).astype(jnp.float32), axis=0)
    squares = jnp.sum(mine * mine, axis=1)
    square_parts = lax.all_to_all(
        jnp.broadcast_to(squares[None], (kv_size,) + squares.shape), "kv", 0, 0, tiled=False
    )
    mean_square = jnp.sum(square_parts, axis=0) / D
    normed = mine * lax.rsqrt(mean_square + norm_eps)[:, None] * post_gain[None, :]
    suffix_hidden = (suffix_resid.astype(jnp.float32) + normed[:tok_rows]).astype(jnp.bfloat16)
    decode_hidden = (decode_resid.astype(jnp.float32) + normed[tok_rows:]).astype(jnp.bfloat16)
    return (suffix_hidden, decode_hidden, new_cache)


def solution(mesh):
    placed = (
        P("blk", "kv"),
        P(None, "blk", "kv"),
        P("blk", "kv"),
        P("blk", "kv"),
        P(None, "blk", "kv"),
        P("blk", "kv"),
        P("kv", None),
        P("kv"),
        P(None, "blk", None, "kv"),
        P(),
        P(None, "blk", None, "kv"),
        P(),
        P(),
        P(),
        P(),
    )
    return jax.shard_map(
        body,
        mesh=mesh,
        in_specs=placed,
        out_specs=(P("blk", "kv"), P("blk", "kv"), P(None, "blk", None, "kv")),
        check_vma=False,
    )
```

```python
import functools
import math

import jax
import jax.numpy as jnp
from jax import lax
from jax.experimental import pallas as pl
from jax.experimental.pallas import tpu as pltpu
from jax.sharding import PartitionSpec as P

D = 4608
QUERY_HEADS = 32
HEAD_SIZE = 128
PAGE_TOKENS = 128
PREFIX_LENGTH = 3072
SLOT_CAPACITY = 1024


soft_cap = 50.0
norm_eps = 1e-06


def prefix_kernel(q_ref, k_ref, v_ref, own_ref, row_ref, num_ref, den_ref, *, q_scale, group):
    step = pl.program_id(1)

    @pl.when(step == 0)
    def _():
        num_ref[...] = jnp.zeros_like(num_ref)
        den_ref[...] = jnp.zeros_like(den_ref)

    q = q_ref[0]
    rows = row_ref[...]
    numer = num_ref[0]
    denom = den_ref[0]
    for part in range(group):
        k = k_ref[part, 0, 0]
        v = v_ref[part, 0, 0]
        s = lax.dot_general(q, k, (((1,), (1,)), ((), ())), preferred_element_type=jnp.float32)
        capped = soft_cap * jnp.tanh(s * (q_scale / soft_cap))
        seen = rows == own_ref[part]
        w = jnp.where(seen, jnp.exp(capped), 0.0)
        for lane in range(0, w.shape[1], 128):
            denom = denom + w[:, lane : lane + 128]
        numer = numer + jnp.dot(w.astype(jnp.bfloat16), v, preferred_element_type=jnp.float32)
    num_ref[0] = numer
    den_ref[0] = denom


def prefix_attention(q_heads, gathered, key_owner, row_prefix, q_scale, group=16):
    heads, rows_q, head_dim = q_heads.shape
    sources, _, _, held_rows, _ = gathered.shape
    steps = sources // group
    kern = functools.partial(prefix_kernel, q_scale=q_scale, group=group)
    return pl.pallas_call(
        kern,
        grid=(heads, steps),
        in_specs=[
            pl.BlockSpec((1, rows_q, head_dim), lambda h, j: (h, 0, 0)),
            pl.BlockSpec((group, 1, 1, held_rows, head_dim), lambda h, j: (j, 0, h, 0, 0)),
            pl.BlockSpec((group, 1, 1, held_rows, head_dim), lambda h, j: (j, 1, h, 0, 0)),
            pl.BlockSpec((group, 1, held_rows), lambda h, j: (j, 0, 0)),
            pl.BlockSpec((rows_q, 1), lambda h, j: (0, 0)),
        ],
        out_specs=[
            pl.BlockSpec((1, rows_q, head_dim), lambda h, j: (h, 0, 0)),
            pl.BlockSpec((1, rows_q, 128), lambda h, j: (h, 0, 0)),
        ],
        out_shape=[
            jax.ShapeDtypeStruct((heads, rows_q, head_dim), jnp.float32),
            jax.ShapeDtypeStruct((heads, rows_q, 128), jnp.float32),
        ],
        compiler_params=pltpu.CompilerParams(dimension_semantics=("parallel", "arbitrary")),
    )(q_heads, gathered, gathered, key_owner, row_prefix)


def from_behind(block, axis, distance):
    devices = range(lax.axis_size(axis))
    route = [(i - distance, i) for i in devices if i - distance in devices]
    return lax.ppermute(block, axis, route)


def attend(query_rows, key_rows, value_rows, visible, q_scale):
    logits = (
        jnp.einsum("qhgd,khd->qhgk", query_rows, key_rows, preferred_element_type=jnp.float32)
        * q_scale
    )
    capped = soft_cap * jnp.tanh(logits / soft_cap)
    weights = jnp.where(visible, jnp.exp(capped), 0.0)
    denominator = jnp.sum(weights, axis=3)
    numerator = jnp.einsum(
        "qhgk,khd->qhgd",
        weights.astype(jnp.bfloat16),
        value_rows,
        preferred_element_type=jnp.float32,
    )
    return (numerator, denominator)


def token_tables(lengths, prefix_ids, token_ids):
    suffix_ends = jnp.cumsum(lengths)
    starts = suffix_ends - lengths
    inside = (
        (token_ids[:, None] >= starts[None, :]) & (token_ids[:, None] < suffix_ends[None, :])
    ).astype(jnp.int32)
    tok_start = jnp.sum(inside * starts[None, :], axis=1)
    tok_prefix = jnp.sum(inside * prefix_ids[None, :], axis=1)
    return (tok_start, tok_prefix)


def inverse_rows(table, wanted):
    hits = (table[None, :] == wanted[:, None]).astype(jnp.int32)
    places = jnp.arange(table.shape[0], dtype=jnp.int32)
    return jnp.sum(hits * places[None, :], axis=1)


def body(
    suffix_query,
    suffix_key_value,
    suffix_resid,
    decode_query_rows,
    decode_key_value,
    decode_resid,
    out_weight,
    post_gain,
    prefix_page_store,
    prefix_table,
    decode_page_store,
    page_table,
    suffix_lengths,
    suffix_prefix,
    decode_ages,
):
    head_dim = HEAD_SIZE
    page_len = PAGE_TOKENS
    q_scale = (D // QUERY_HEADS) ** (-0.5)
    tok_rows = suffix_query.shape[0]
    q_heads = suffix_query.shape[1] // head_dim
    kv_heads = suffix_key_value.shape[2] // head_dim
    query_group_width = q_heads // kv_heads
    blk_size = lax.axis_size("blk")
    my_index = lax.axis_index("blk")

    local_pages = prefix_page_store.shape[1]
    dq_rows = decode_query_rows.shape[0]
    kv_width = kv_heads * head_dim
    dq_lines = decode_query_rows.size // kv_width
    dkv_lines = decode_key_value.size // kv_width
    dec_local = jnp.concatenate(
        [
            decode_query_rows.reshape(dq_lines, kv_width),
            decode_key_value.reshape(dkv_lines, kv_width),
        ],
        axis=0,
    )
    dec_all = lax.all_to_all(
        jnp.broadcast_to(dec_local[None], (blk_size,) + dec_local.shape), "blk", 0, 0, tiled=False
    )
    all_dq = dec_all[:, :dq_lines].reshape(blk_size * dq_rows, q_heads * head_dim)
    all_dkv = (
        dec_all[:, dq_lines:]
        .reshape(blk_size, 2, dq_rows, kv_width)
        .transpose(1, 0, 2, 3)
        .reshape(2, blk_size * dq_rows, kv_width)
    )

    held_rows = local_pages * page_len
    piece = prefix_page_store.reshape(2, held_rows, kv_heads, head_dim).transpose(0, 2, 1, 3)
    gathered = lax.all_gather(piece, "blk", axis=0, tiled=False)

    look_back = 4
    pieces_back = [from_behind(suffix_key_value, "blk", d) for d in range(look_back, 0, -1)]
    window = jnp.concatenate(pieces_back + [suffix_key_value], axis=1)

    own_queries = suffix_query.reshape(tok_rows, kv_heads, query_group_width, head_dim)
    token_ids = my_index * tok_rows + jnp.arange(tok_rows, dtype=jnp.int32)
    tok_start, tok_prefix = token_tables(suffix_lengths, suffix_prefix, token_ids)
    key_ids = (my_index - look_back) * tok_rows + jnp.arange(
        (look_back + 1) * tok_rows, dtype=jnp.int32
    )
    visible = (key_ids[None, :] >= tok_start[:, None]) & (key_ids[None, :] <= token_ids[:, None])
    window_keys = window[0].reshape((look_back + 1) * tok_rows, kv_heads, head_dim)
    window_values = window[1].reshape((look_back + 1) * tok_rows, kv_heads, head_dim)
    own_numer, own_denom = attend(
        own_queries, window_keys, window_values, visible[:, None, None, :], q_scale
    )

    pool_pages = prefix_table.shape[0]
    per_prefix = PREFIX_LENGTH // PAGE_TOKENS
    page_owner = inverse_rows(prefix_table, jnp.arange(pool_pages, dtype=jnp.int32)) // per_prefix
    key_owner = jnp.repeat(page_owner, page_len).reshape(blk_size, 1, held_rows)
    row_prefix = jnp.repeat(tok_prefix, query_group_width)[:, None]
    rows_q = tok_rows * query_group_width
    q_by_head = own_queries.transpose(1, 0, 2, 3).reshape(kv_heads, rows_q, head_dim)
    numer_p, denom_lanes = prefix_attention(q_by_head, gathered, key_owner, row_prefix, q_scale)
    denom_p = jnp.sum(denom_lanes, axis=2)
    pre_numer = numer_p.reshape(kv_heads, tok_rows, query_group_width, head_dim).transpose(
        1, 0, 2, 3
    )
    pre_denom = denom_p.reshape(kv_heads, tok_rows, query_group_width).transpose(1, 0, 2)
    suffix_attn = ((own_numer + pre_numer) / (own_denom + pre_denom)[..., None]).astype(
        jnp.bfloat16
    )
    suffix_attn = suffix_attn.reshape(tok_rows, q_heads * head_dim)

    slot_total = all_dq.shape[0]
    slot_pages = SLOT_CAPACITY // PAGE_TOKENS
    local_cache = decode_page_store.shape[1]
    page_ids = my_index * local_cache + jnp.arange(local_cache, dtype=jnp.int32)
    position = inverse_rows(page_table, page_ids)
    slot_of = position // slot_pages
    block_of = position % slot_pages
    slot_hot = slot_of[:, None] == jnp.arange(slot_total, dtype=jnp.int32)[None, :]
    page_age = jnp.sum(slot_hot.astype(jnp.int32) * decode_ages[None, :], axis=1)
    select = slot_hot.astype(jnp.bfloat16)
    new_rows = jnp.einsum(
        "ls,tsc->tlc", select, all_dkv, preferred_element_type=jnp.float32
    ).astype(jnp.bfloat16)
    write_here = (block_of == page_age // page_len)[:, None] & (
        jnp.arange(page_len, dtype=jnp.int32)[None, :] == (page_age % page_len)[:, None]
    )
    new_cache = jnp.where(write_here[None, :, :, None], new_rows[:, :, None, :], decode_page_store)
    page_queries = jnp.dot(select, all_dq, preferred_element_type=jnp.float32).astype(jnp.bfloat16)
    page_queries = page_queries.reshape(local_cache, kv_heads, query_group_width, head_dim)
    key_cache = new_cache[0].reshape(local_cache, page_len, kv_heads, head_dim)
    value_cache = new_cache[1].reshape(local_cache, page_len, kv_heads, head_dim)
    logits = (
        jnp.einsum("lhgd,lphd->lhgp", page_queries, key_cache, preferred_element_type=jnp.float32)
        * q_scale
    )
    capped = soft_cap * jnp.tanh(logits / soft_cap)
    places = block_of[:, None] * page_len + jnp.arange(page_len, dtype=jnp.int32)[None, :]
    seen_pos = places <= page_age[:, None]
    weights = jnp.where(seen_pos[:, None, None, :], jnp.exp(capped), 0.0)
    page_denom = jnp.sum(weights, axis=3)
    page_numer = jnp.einsum(
        "lhgp,lphd->lhgd",
        weights.astype(jnp.bfloat16),
        value_cache,
        preferred_element_type=jnp.float32,
    )
    slot_float = slot_hot.astype(jnp.float32)
    page_sums = jnp.concatenate([page_numer, page_denom[..., None]], axis=3)
    slot_sums = jnp.einsum("ls,lhgd->shgd", slot_float, page_sums, precision=lax.Precision.HIGHEST)
    slot_sums = slot_sums.reshape((blk_size, slot_total // blk_size) + slot_sums.shape[1:])
    mine_sums = jnp.sum(lax.all_to_all(slot_sums, "blk", 0, 0, tiled=False), axis=0)
    mine_numer = mine_sums[..., :head_dim]
    mine_denom = mine_sums[..., head_dim]
    decode_attn = (mine_numer / mine_denom[..., None]).astype(jnp.bfloat16)
    decode_rows = decode_attn.shape[0]
    decode_attn = decode_attn.reshape(decode_rows, q_heads * head_dim)

    attention = jnp.concatenate([suffix_attn, decode_attn], axis=0)
    kv_size = lax.axis_size("kv")
    weight_blocks = out_weight.reshape(out_weight.shape[0], kv_size, -1)
    shares = jnp.einsum(
        "rk,kdo->dro", attention, weight_blocks, preferred_element_type=jnp.float32
    ).astype(jnp.bfloat16)
    mine = jnp.sum(lax.all_to_all(shares, "kv", 0, 0, tiled=False).astype(jnp.float32), axis=0)
    squares = jnp.sum(mine * mine, axis=1)
    square_parts = lax.all_to_all(
        jnp.broadcast_to(squares[None], (kv_size,) + squares.shape), "kv", 0, 0, tiled=False
    )
    mean_square = jnp.sum(square_parts, axis=0) / D
    normed = mine * lax.rsqrt(mean_square + norm_eps)[:, None] * post_gain[None, :]
    suffix_hidden = (suffix_resid.astype(jnp.float32) + normed[:tok_rows]).astype(jnp.bfloat16)
    decode_hidden = (decode_resid.astype(jnp.float32) + normed[tok_rows:]).astype(jnp.bfloat16)
    return (suffix_hidden, decode_hidden, new_cache)


def solution(mesh):
    placed = (
        P("blk", "kv"),
        P(None, "blk", "kv"),
        P("blk", "kv"),
        P("blk", "kv"),
        P(None, "blk", "kv"),
        P("blk", "kv"),
        P("kv", None),
        P("kv"),
        P(None, "blk", None, "kv"),
        P(),
        P(None, "blk", None, "kv"),
        P(),
        P(),
        P(),
        P(),
    )
    return jax.shard_map(
        body,
        mesh=mesh,
        in_specs=placed,
        out_specs=(P("blk", "kv"), P("blk", "kv"), P(None, "blk", None, "kv")),
        check_vma=False,
    )
```

```python
import functools
import math

import jax
import jax.numpy as jnp
from jax import lax
from jax.experimental import pallas as pl
from jax.experimental.pallas import tpu as pltpu
from jax.sharding import PartitionSpec as P

D = 4608
QUERY_HEADS = 32
HEAD_SIZE = 128
PAGE_TOKENS = 128
PREFIX_LENGTH = 3072
SLOT_CAPACITY = 1024


soft_cap = 50.0
norm_eps = 1e-06


def prefix_kernel(q_ref, k_ref, v_ref, own_ref, row_ref, num_ref, den_ref, *, q_scale, group):
    step = pl.program_id(1)

    @pl.when(step == 0)
    def _():
        num_ref[...] = jnp.zeros_like(num_ref)
        den_ref[...] = jnp.zeros_like(den_ref)

    q = q_ref[0]
    rows = row_ref[...]
    numer = num_ref[0]
    denom = den_ref[0]
    for part in range(group):
        k = k_ref[part, 0, 0]
        v = v_ref[part, 0, 0]
        s = lax.dot_general(q, k, (((1,), (1,)), ((), ())), preferred_element_type=jnp.float32)
        capped = soft_cap * jnp.tanh(s * (q_scale / soft_cap))
        seen = rows == own_ref[part]
        w = jnp.where(seen, jnp.exp(capped), 0.0)
        denom = denom + jnp.sum(w, axis=1, keepdims=True)
        numer = numer + jnp.dot(w.astype(jnp.bfloat16), v, preferred_element_type=jnp.float32)
    num_ref[0] = numer
    den_ref[0] = denom


def prefix_attention(q_heads, gathered, key_owner, row_prefix, q_scale, group=32):
    heads, rows_q, head_dim = q_heads.shape
    sources, _, _, held_rows, _ = gathered.shape
    steps = sources // group
    kern = functools.partial(prefix_kernel, q_scale=q_scale, group=group)
    return pl.pallas_call(
        kern,
        grid=(heads, steps),
        in_specs=[
            pl.BlockSpec((1, rows_q, head_dim), lambda h, j: (h, 0, 0)),
            pl.BlockSpec((group, 1, 1, held_rows, head_dim), lambda h, j: (j, 0, h, 0, 0)),
            pl.BlockSpec((group, 1, 1, held_rows, head_dim), lambda h, j: (j, 1, h, 0, 0)),
            pl.BlockSpec((group, 1, held_rows), lambda h, j: (j, 0, 0)),
            pl.BlockSpec((rows_q, 1), lambda h, j: (0, 0)),
        ],
        out_specs=[
            pl.BlockSpec((1, rows_q, head_dim), lambda h, j: (h, 0, 0)),
            pl.BlockSpec((1, rows_q, 1), lambda h, j: (h, 0, 0)),
        ],
        out_shape=[
            jax.ShapeDtypeStruct((heads, rows_q, head_dim), jnp.float32),
            jax.ShapeDtypeStruct((heads, rows_q, 1), jnp.float32),
        ],
        compiler_params=pltpu.CompilerParams(dimension_semantics=("parallel", "arbitrary")),
    )(q_heads, gathered, gathered, key_owner, row_prefix)


def from_behind(block, axis, distance):
    devices = range(lax.axis_size(axis))
    route = [(i - distance, i) for i in devices if i - distance in devices]
    return lax.ppermute(block, axis, route)


def attend(query_rows, key_rows, value_rows, visible, q_scale):
    logits = (
        jnp.einsum("qhgd,khd->qhgk", query_rows, key_rows, preferred_element_type=jnp.float32)
        * q_scale
    )
    capped = soft_cap * jnp.tanh(logits / soft_cap)
    weights = jnp.where(visible, jnp.exp(capped), 0.0)
    denominator = jnp.sum(weights, axis=3)
    numerator = jnp.einsum(
        "qhgk,khd->qhgd",
        weights.astype(jnp.bfloat16),
        value_rows,
        preferred_element_type=jnp.float32,
    )
    return (numerator, denominator)


def token_tables(lengths, prefix_ids, token_ids):
    suffix_ends = jnp.cumsum(lengths)
    starts = suffix_ends - lengths
    inside = (
        (token_ids[:, None] >= starts[None, :]) & (token_ids[:, None] < suffix_ends[None, :])
    ).astype(jnp.int32)
    tok_start = jnp.sum(inside * starts[None, :], axis=1)
    tok_prefix = jnp.sum(inside * prefix_ids[None, :], axis=1)
    return (tok_start, tok_prefix)


def inverse_rows(table, wanted):
    hits = (table[None, :] == wanted[:, None]).astype(jnp.int32)
    places = jnp.arange(table.shape[0], dtype=jnp.int32)
    return jnp.sum(hits * places[None, :], axis=1)


def body(
    suffix_query,
    suffix_key_value,
    suffix_resid,
    decode_query_rows,
    decode_key_value,
    decode_resid,
    out_weight,
    post_gain,
    prefix_page_store,
    prefix_table,
    decode_page_store,
    page_table,
    suffix_lengths,
    suffix_prefix,
    decode_ages,
):
    head_dim = HEAD_SIZE
    page_len = PAGE_TOKENS
    q_scale = (D // QUERY_HEADS) ** (-0.5)
    tok_rows = suffix_query.shape[0]
    q_heads = suffix_query.shape[1] // head_dim
    kv_heads = suffix_key_value.shape[2] // head_dim
    query_group_width = q_heads // kv_heads
    blk_size = lax.axis_size("blk")
    my_index = lax.axis_index("blk")

    local_pages = prefix_page_store.shape[1]
    dq_rows = decode_query_rows.shape[0]
    kv_width = kv_heads * head_dim
    dq_lines = decode_query_rows.size // kv_width
    dkv_lines = decode_key_value.size // kv_width
    dec_local = jnp.concatenate(
        [
            decode_query_rows.reshape(dq_lines, kv_width),
            decode_key_value.reshape(dkv_lines, kv_width),
        ],
        axis=0,
    )
    dec_all = lax.all_to_all(
        jnp.broadcast_to(dec_local[None], (blk_size,) + dec_local.shape), "blk", 0, 0, tiled=False
    )
    all_dq = dec_all[:, :dq_lines].reshape(blk_size * dq_rows, q_heads * head_dim)
    all_dkv = (
        dec_all[:, dq_lines:]
        .reshape(blk_size, 2, dq_rows, kv_width)
        .transpose(1, 0, 2, 3)
        .reshape(2, blk_size * dq_rows, kv_width)
    )

    held_rows = local_pages * page_len
    piece = prefix_page_store.reshape(2, held_rows, kv_heads, head_dim).transpose(0, 2, 1, 3)
    gathered = lax.all_gather(piece, "blk", axis=0, tiled=False)

    look_back = 4
    pieces_back = [from_behind(suffix_key_value, "blk", d) for d in range(look_back, 0, -1)]
    window = jnp.concatenate(pieces_back + [suffix_key_value], axis=1)

    own_queries = suffix_query.reshape(tok_rows, kv_heads, query_group_width, head_dim)
    token_ids = my_index * tok_rows + jnp.arange(tok_rows, dtype=jnp.int32)
    tok_start, tok_prefix = token_tables(suffix_lengths, suffix_prefix, token_ids)
    key_ids = (my_index - look_back) * tok_rows + jnp.arange(
        (look_back + 1) * tok_rows, dtype=jnp.int32
    )
    visible = (key_ids[None, :] >= tok_start[:, None]) & (key_ids[None, :] <= token_ids[:, None])
    window_keys = window[0].reshape((look_back + 1) * tok_rows, kv_heads, head_dim)
    window_values = window[1].reshape((look_back + 1) * tok_rows, kv_heads, head_dim)
    own_numer, own_denom = attend(
        own_queries, window_keys, window_values, visible[:, None, None, :], q_scale
    )

    pool_pages = prefix_table.shape[0]
    per_prefix = PREFIX_LENGTH // PAGE_TOKENS
    page_owner = inverse_rows(prefix_table, jnp.arange(pool_pages, dtype=jnp.int32)) // per_prefix
    key_owner = jnp.repeat(page_owner, page_len).reshape(blk_size, 1, held_rows)
    row_prefix = jnp.repeat(tok_prefix, query_group_width)[:, None]
    rows_q = tok_rows * query_group_width
    q_by_head = own_queries.transpose(1, 0, 2, 3).reshape(kv_heads, rows_q, head_dim)
    numer_p, denom_p = prefix_attention(q_by_head, gathered, key_owner, row_prefix, q_scale)
    pre_numer = numer_p.reshape(kv_heads, tok_rows, query_group_width, head_dim).transpose(
        1, 0, 2, 3
    )
    pre_denom = denom_p.reshape(kv_heads, tok_rows, query_group_width).transpose(1, 0, 2)
    suffix_attn = ((own_numer + pre_numer) / (own_denom + pre_denom)[..., None]).astype(
        jnp.bfloat16
    )
    suffix_attn = suffix_attn.reshape(tok_rows, q_heads * head_dim)

    slot_total = all_dq.shape[0]
    slot_pages = SLOT_CAPACITY // PAGE_TOKENS
    local_cache = decode_page_store.shape[1]
    page_ids = my_index * local_cache + jnp.arange(local_cache, dtype=jnp.int32)
    position = inverse_rows(page_table, page_ids)
    slot_of = position // slot_pages
    block_of = position % slot_pages
    slot_hot = slot_of[:, None] == jnp.arange(slot_total, dtype=jnp.int32)[None, :]
    page_age = jnp.sum(slot_hot.astype(jnp.int32) * decode_ages[None, :], axis=1)
    select = slot_hot.astype(jnp.bfloat16)
    new_rows = jnp.einsum(
        "ls,tsc->tlc", select, all_dkv, preferred_element_type=jnp.float32
    ).astype(jnp.bfloat16)
    write_here = (block_of == page_age // page_len)[:, None] & (
        jnp.arange(page_len, dtype=jnp.int32)[None, :] == (page_age % page_len)[:, None]
    )
    new_cache = jnp.where(write_here[None, :, :, None], new_rows[:, :, None, :], decode_page_store)
    page_queries = jnp.dot(select, all_dq, preferred_element_type=jnp.float32).astype(jnp.bfloat16)
    page_queries = page_queries.reshape(local_cache, kv_heads, query_group_width, head_dim)
    key_cache = new_cache[0].reshape(local_cache, page_len, kv_heads, head_dim)
    value_cache = new_cache[1].reshape(local_cache, page_len, kv_heads, head_dim)
    logits = (
        jnp.einsum("lhgd,lphd->lhgp", page_queries, key_cache, preferred_element_type=jnp.float32)
        * q_scale
    )
    capped = soft_cap * jnp.tanh(logits / soft_cap)
    places = block_of[:, None] * page_len + jnp.arange(page_len, dtype=jnp.int32)[None, :]
    seen_pos = places <= page_age[:, None]
    weights = jnp.where(seen_pos[:, None, None, :], jnp.exp(capped), 0.0)
    page_denom = jnp.sum(weights, axis=3)
    page_numer = jnp.einsum(
        "lhgp,lphd->lhgd",
        weights.astype(jnp.bfloat16),
        value_cache,
        preferred_element_type=jnp.float32,
    )
    slot_float = slot_hot.astype(jnp.float32)
    page_sums = jnp.concatenate([page_numer, page_denom[..., None]], axis=3)
    slot_sums = jnp.einsum("ls,lhgd->shgd", slot_float, page_sums, precision=lax.Precision.HIGHEST)
    slot_sums = slot_sums.reshape((blk_size, slot_total // blk_size) + slot_sums.shape[1:])
    mine_sums = jnp.sum(lax.all_to_all(slot_sums, "blk", 0, 0, tiled=False), axis=0)
    mine_numer = mine_sums[..., :head_dim]
    mine_denom = mine_sums[..., head_dim]
    decode_attn = (mine_numer / mine_denom[..., None]).astype(jnp.bfloat16)
    decode_rows = decode_attn.shape[0]
    decode_attn = decode_attn.reshape(decode_rows, q_heads * head_dim)

    attention = jnp.concatenate([suffix_attn, decode_attn], axis=0)
    kv_size = lax.axis_size("kv")
    weight_blocks = out_weight.reshape(out_weight.shape[0], kv_size, -1)
    shares = jnp.einsum(
        "rk,kdo->dro", attention, weight_blocks, preferred_element_type=jnp.float32
    ).astype(jnp.bfloat16)
    mine = jnp.sum(lax.all_to_all(shares, "kv", 0, 0, tiled=False).astype(jnp.float32), axis=0)
    squares = jnp.sum(mine * mine, axis=1)
    square_parts = lax.all_to_all(
        jnp.broadcast_to(squares[None], (kv_size,) + squares.shape), "kv", 0, 0, tiled=False
    )
    mean_square = jnp.sum(square_parts, axis=0) / D
    normed = mine * lax.rsqrt(mean_square + norm_eps)[:, None] * post_gain[None, :]
    suffix_hidden = (suffix_resid.astype(jnp.float32) + normed[:tok_rows]).astype(jnp.bfloat16)
    decode_hidden = (decode_resid.astype(jnp.float32) + normed[tok_rows:]).astype(jnp.bfloat16)
    return (suffix_hidden, decode_hidden, new_cache)


def solution(mesh):
    placed = (
        P("blk", "kv"),
        P(None, "blk", "kv"),
        P("blk", "kv"),
        P("blk", "kv"),
        P(None, "blk", "kv"),
        P("blk", "kv"),
        P("kv", None),
        P("kv"),
        P(None, "blk", None, "kv"),
        P(),
        P(None, "blk", None, "kv"),
        P(),
        P(),
        P(),
        P(),
    )
    return jax.shard_map(
        body,
        mesh=mesh,
        in_specs=placed,
        out_specs=(P("blk", "kv"), P("blk", "kv"), P(None, "blk", None, "kv")),
        check_vma=False,
    )
```
